128 devices in a mesh: rep: 16 (over z_lo, x, core), shard: 8 (over z_hi, y).
Axes of the slice: x: 4, y: 4, z: 4 (z_hi: 2, z_lo: 2; z = z_hi * 2 + z_lo), core: 2. Of those that a mesh axis runs over, the one named last changes fastest.
Arguments:
- grad_embed: bfloat16 [16, 8, 4096, 768], P('rep', 'shard'), may hold values from -800 to 800
- grad_proj: bfloat16 [16, 8, 768, 768], P('rep', 'shard'), may hold values from -800 to 800
- grad_norms: bfloat16 [16, 8, 4, 768], P('rep', 'shard'), may hold values from -800 to 800
- embed_master: float32 [4096, 768], P('shard'), may hold values from -0.75 to 0.75
- embed_first: float32 [4096, 768], P('shard'), may hold values from -6 to 6
- embed_second: float32 [4096, 768], P('shard'), may hold values from 0.01 to 4
- proj_master: float32 [768, 768], P('shard'), may hold values from -0.21875 to 0.21875
- proj_first: float32 [768, 768], P('shard'), may hold values from -6 to 6
- proj_second: float32 [768, 768], P('shard'), may hold values from 0.01 to 4
- norm_master: float32 [4, 768], P(None, 'shard'), may hold values from -6 to 6
- norm_first: float32 [4, 768], P(None, 'shard'), may hold values from -6 to 6
- norm_second: float32 [4, 768], P(None, 'shard'), may hold values from 0.01 to 4
Outputs:
- embed_master_new: float32 [4096, 768], P('shard')
- embed_first_new: float32 [4096, 768], P('shard')
- embed_second_new: float32 [4096, 768], P('shard')
- embed_weights: bfloat16 [4096, 768], replicated
- proj_master_new: float32 [768, 768], P('shard')
- proj_first_new: float32 [768, 768], P('shard')
- proj_second_new: float32 [768, 768], P('shard')
- proj_weights: bfloat16 [768, 768], replicated
- norm_master_new: float32 [4, 768], P(None, 'shard')
- norm_first_new: float32 [4, 768], P(None, 'shard')
- norm_second_new: float32 [4, 768], P(None, 'shard')
- norm_weights: bfloat16 [4, 768], replicated
The draws below stay inside these ranges and needn't reach their ends.
All inputs are finite; a program needn't handle non-finite values.
Results may differ from the reference program's by a relative error of at most 0.0004.
Values may be sent and summed in bfloat16 or wider, within the bound.
No kernel may reach another device: no remote copies, remote signals or barrier semaphores. Data moves between devices by JAX's collectives and lax.ppermute only.
A program may use at most 128 MiB of HBM per device.

```python
import math
import jax
import jax.numpy as jnp
from jax import lax

D = 768
EMB = 4096
N_REP = 16
N_SHARD = 8


def rough_grad(key, row_count, col_count, band_rows):
    first_key = jax.random.fold_in(key, 0)
    second_key = jax.random.fold_in(key, 1)
    fourth_key = jax.random.fold_in(key, 3)
    full_shape = (N_REP, N_SHARD, row_count, col_count)
    row_scale = 10.0 ** jax.random.uniform(second_key, (row_count, 1), jnp.float32)
    col_scale = 10.0 ** jax.random.uniform(fourth_key, (1, col_count), jnp.float32)
    shard_index = jnp.arange(N_SHARD, dtype=jnp.int32)[None, :, None, None]
    if band_rows:
        band_index = (jnp.arange(row_count, dtype=jnp.int32) // (row_count // N_SHARD))[None, None, :, None]
    else:
        band_index = (jnp.arange(col_count, dtype=jnp.int32) // (col_count // N_SHARD))[None, None, None, :]
    band_boost = jnp.where(band_index == shard_index, 3.0, 1.0).astype(jnp.float32)
    band_level = band_index.astype(jnp.float32) / float(max(N_SHARD - 1, 1))
    band_rise = (1.0 + 2.0 * band_level) / 3.0
    base_values = 0.5 * jnp.clip(jax.random.normal(first_key, full_shape, jnp.float32), -5.0, 5.0)
    return (base_values * band_rise * band_boost * row_scale * col_scale).astype(jnp.bfloat16)


def draw_grad_embed(key, part):
    return rough_grad(jax.random.fold_in(key, 11), EMB, D, True)


def draw_grad_proj(key, part):
    return rough_grad(jax.random.fold_in(key, 12), D, D, True)


def draw_grad_norms(key, part):
    return rough_grad(jax.random.fold_in(key, 13), 4, D, False)


def levels(stream_key, shape, shards, low, high):
    def one(dim, shards_of):
        steps = jax.random.uniform(jax.random.fold_in(jax.random.fold_in(stream_key, 6), dim), (shards_of,), jnp.float32, low / len(shards), high / len(shards))
        return jnp.repeat(jnp.exp(steps), shape[dim] // shards_of).reshape((-1,) + (1,) * (len(shape) - dim - 1))

    gain = one(*shards[0])
    for cut in shards[1:]:
        gain = gain * one(*cut)
    return gain


def scatter_about(stream_key, extent, spread, reach, shards=(), held_as=jnp.bfloat16):
    drawn = jax.random.normal(stream_key, extent, jnp.float32) * spread
    if len(shards) > 0:
        drawn = levels(stream_key, extent, shards, -0.22, 0.18) * drawn
    return jnp.clip(drawn, min=-reach, max=reach).astype(held_as)


def setup_inputs(seed: int = 0) -> dict:
    key_of = jax.random.split(jax.random.key(seed), 13)
    return {
        "grad_embed": draw_grad_embed(jax.random.fold_in(key_of[12], 71), 0),
        "grad_proj": draw_grad_proj(jax.random.fold_in(key_of[12], 71), 0),
        "grad_norms": draw_grad_norms(jax.random.fold_in(key_of[12], 71), 0),
        "embed_master": scatter_about(key_of[3], (EMB, D), 0.05, 0.75, ((0, 8),), jnp.float32),
        "embed_first": scatter_about(key_of[4], (EMB, D), 0.5, 6.0, ((0, 8),), jnp.float32),
        "embed_second": jnp.clip(jnp.exp(math.log(4.0) - 5.9914646 * jax.random.uniform(key_of[5], (EMB, D), jnp.float32) ** levels(key_of[5], (EMB, D), ((0, 8),), -0.2, 0.2)), 0.01, 4.0),
        "proj_master": scatter_about(key_of[6], (D, D), D ** -0.5, 0.21875, ((0, 8),), jnp.float32),
        "proj_first": scatter_about(key_of[7], (D, D), 0.5, 6.0, ((0, 8),), jnp.float32),
        "proj_second": jnp.clip(jnp.exp(math.log(4.0) - 5.9914646 * jax.random.uniform(key_of[8], (D, D), jnp.float32) ** levels(key_of[8], (D, D), ((0, 8),), -0.2, 0.2)), 0.01, 4.0),
        "norm_master": scatter_about(key_of[9], (4, D), 0.5, 6.0, ((1, 8),), jnp.float32),
        "norm_first": scatter_about(key_of[10], (4, D), 0.5, 6.0, ((1, 8),), jnp.float32),
        "norm_second": jnp.clip(jnp.exp(math.log(4.0) - 5.9914646 * jax.random.uniform(key_of[11], (4, D), jnp.float32) ** levels(key_of[11], (4, D), ((1, 8),), -0.2, 0.2)), 0.01, 4.0),
    }


beta_one = 0.9
beta_two = 0.95
adam_step = 10.0
adam_eps = 1e-08
learning_rate = 0.002
clip_rms = 1.0

def accumulate(grads):
    flat = grads.reshape((-1,) + grads.shape[2:])

    def add_term(running, device_term):
        return (running + device_term.astype(jnp.float32), None)
    running, _ = lax.scan(add_term, jnp.zeros(grads.shape[2:], jnp.float32), flat)
    return running

def adamw(gradient, master, first, second, weight_decay):
    corr_one = 1.0 - beta_one ** adam_step
    corr_two = 1.0 - beta_two ** adam_step
    first_new = beta_one * first + (1.0 - beta_one) * gradient
    second_new = beta_two * second + (1.0 - beta_two) * gradient * gradient
    direction = first_new / corr_one / (jnp.sqrt(second_new / corr_two) + adam_eps) + weight_decay * master
    master_new = master - learning_rate * direction
    return (master_new, first_new, second_new, master_new.astype(jnp.bfloat16))

def reference(grad_embed, grad_proj, grad_norms, embed_master, embed_first, embed_second, proj_master, proj_first, proj_second, norm_master, norm_first, norm_second):
    embed_sum = accumulate(grad_embed)
    proj_sum = accumulate(grad_proj)
    norm_sum = accumulate(grad_norms)
    squares = jnp.sum(embed_sum * embed_sum) + jnp.sum(proj_sum * proj_sum) + jnp.sum(norm_sum * norm_sum)
    entry_count = float(EMB * D + D * D + 4 * D)
    rms_value = jnp.sqrt(squares / entry_count)
    clip_factor = jnp.minimum(jnp.float32(1.0), clip_rms / (rms_value + 1e-06))
    embed_out = adamw(clip_factor * embed_sum, embed_master, embed_first, embed_second, 0.01)
    proj_out = adamw(clip_factor * proj_sum, proj_master, proj_first, proj_second, 0.01)
    norm_out = adamw(clip_factor * norm_sum, norm_master, norm_first, norm_second, 0.0)
    return (embed_out[0], embed_out[1], embed_out[2], embed_out[3], proj_out[0], proj_out[1], proj_out[2], proj_out[3], norm_out[0], norm_out[1], norm_out[2], norm_out[3])
```

```python
import jax
import jax.numpy as jnp
from jax import lax
from jax.sharding import PartitionSpec as P

beta_one = 0.9
beta_two = 0.95
adam_step = 10.0
adam_eps = 1e-08
learning_rate = 0.002
clip_rms = 1.0

ALL = ("shard", "rep")


def adamw(gradient, master, first, second, weight_decay):
    corr_one = 1.0 - beta_one**adam_step
    corr_two = 1.0 - beta_two**adam_step
    first_new = beta_one * first + (1.0 - beta_one) * gradient
    second_new = beta_two * second + (1.0 - beta_two) * gradient * gradient
    direction = (
        first_new / corr_one / (jnp.sqrt(second_new / corr_two) + adam_eps) + weight_decay * master
    )
    master_new = master - learning_rate * direction
    return (master_new, first_new, second_new, master_new.astype(jnp.bfloat16))


def gather_all(piece, axis):
    count = lax.psum(1, axis)
    return lax.all_to_all(
        jnp.broadcast_to(piece[None], (count,) + piece.shape), axis, 0, 0, tiled=True
    )


def shards(
    grad_embed,
    grad_proj,
    grad_norms,
    embed_master,
    embed_first,
    embed_second,
    proj_master,
    proj_first,
    proj_second,
    norm_master,
    norm_first,
    norm_second,
):
    n_rep = lax.psum(1, "rep")
    n_shard = lax.psum(1, "shard")
    n_all = n_rep * n_shard
    rep_index = lax.axis_index("rep")

    embed_rows, width = grad_embed.shape[2:]
    proj_rows = grad_proj.shape[2]
    norm_rows, norm_cols = grad_norms.shape[2:]
    e_rows = embed_rows // n_all
    p_rows = proj_rows // n_all
    n_vals = norm_rows * norm_cols // n_all
    block_norm = norm_cols // n_shard
    rows = e_rows + p_rows + 2
    entry_count = float(embed_rows * width + proj_rows * width + norm_rows * norm_cols)

    embed_send = grad_embed[0, 0].reshape(n_all, e_rows, width)
    proj_send = grad_proj[0, 0].reshape(n_all, p_rows, width)
    norm_send = (
        grad_norms[0, 0]
        .reshape(norm_rows, n_shard, block_norm)
        .transpose(1, 0, 2)
        .reshape(n_all, 1, n_vals)
    )
    norm_send = jnp.pad(norm_send, ((0, 0), (0, 1), (0, width - n_vals)))
    send = jnp.concatenate([embed_send, proj_send, norm_send], axis=1)

    received = lax.all_to_all(send, ALL, 0, 0, tiled=True)
    reduced = jnp.sum(received.astype(jnp.float32), axis=0)

    partial = jnp.sum(reduced * reduced)
    squares = jnp.sum(gather_all(partial.reshape(1), ALL))
    rms_value = jnp.sqrt(squares / entry_count)
    clip_factor = jnp.minimum(jnp.float32(1.0), clip_rms / (rms_value + 1e-06))

    def flat_norm(x):
        return lax.dynamic_slice(x.reshape(-1), (rep_index * n_vals,), (n_vals,))

    e_piece = adamw(
        clip_factor * reduced[:e_rows],
        lax.dynamic_slice_in_dim(embed_master, rep_index * e_rows, e_rows),
        lax.dynamic_slice_in_dim(embed_first, rep_index * e_rows, e_rows),
        lax.dynamic_slice_in_dim(embed_second, rep_index * e_rows, e_rows),
        0.01,
    )[3]
    p_piece = adamw(
        clip_factor * reduced[e_rows : e_rows + p_rows],
        lax.dynamic_slice_in_dim(proj_master, rep_index * p_rows, p_rows),
        lax.dynamic_slice_in_dim(proj_first, rep_index * p_rows, p_rows),
        lax.dynamic_slice_in_dim(proj_second, rep_index * p_rows, p_rows),
        0.01,
    )[3]
    n_piece = adamw(
        clip_factor * reduced[e_rows + p_rows, :n_vals],
        flat_norm(norm_master),
        flat_norm(norm_first),
        flat_norm(norm_second),
        0.0,
    )[3]
    n_piece = jnp.pad(n_piece.reshape(1, n_vals), ((0, 1), (0, width - n_vals)))
    w_piece = jnp.concatenate([e_piece, p_piece, n_piece], axis=0)
    w_all = gather_all(w_piece, ALL)
    embed_weights = w_all[:, :e_rows].reshape(embed_rows, width)
    proj_weights = w_all[:, e_rows : e_rows + p_rows].reshape(proj_rows, width)
    norm_weights = (
        w_all[:, e_rows + p_rows, :n_vals]
        .reshape(n_shard, norm_rows, block_norm)
        .transpose(1, 0, 2)
        .reshape(norm_rows, norm_cols)
    )

    block = gather_all(reduced, "rep")
    embed_sum = block[:, :e_rows].reshape(n_rep * e_rows, width)
    proj_sum = block[:, e_rows : e_rows + p_rows].reshape(n_rep * p_rows, width)
    norm_sum = block[:, e_rows + p_rows, :n_vals].reshape(norm_rows, block_norm)

    embed_out = adamw(clip_factor * embed_sum, embed_master, embed_first, embed_second, 0.01)
    proj_out = adamw(clip_factor * proj_sum, proj_master, proj_first, proj_second, 0.01)
    norm_out = adamw(clip_factor * norm_sum, norm_master, norm_first, norm_second, 0.0)
    return (
        embed_out[0],
        embed_out[1],
        embed_out[2],
        embed_weights,
        proj_out[0],
        proj_out[1],
        proj_out[2],
        proj_weights,
        norm_out[0],
        norm_out[1],
        norm_out[2],
        norm_weights,
    )


def solution(mesh):
    return jax.shard_map(
        shards,
        mesh=mesh,
        in_specs=(
            P("rep", "shard", None, None),
            P("rep", "shard", None, None),
            P("rep", "shard", None, None),
            P("shard", None),
            P("shard", None),
            P("shard", None),
            P("shard", None),
            P("shard", None),
            P("shard", None),
            P(None, "shard"),
            P(None, "shard"),
            P(None, "shard"),
        ),
        out_specs=(
            P("shard", None),
            P("shard", None),
            P("shard", None),
            P(),
            P("shard", None),
            P("shard", None),
            P("shard", None),
            P(),
            P(None, "shard"),
            P(None, "shard"),
            P(None, "shard"),
            P(),
        ),
        check_vma=False,
    )
```

```python
import jax
import jax.numpy as jnp
from jax import lax
from jax.sharding import PartitionSpec as P

beta_one = 0.9
beta_two = 0.95
adam_step = 10.0
adam_eps = 1e-08
learning_rate = 0.002
clip_rms = 1.0

ALL = ("shard", "rep")


def adamw(gradient, master, first, second, weight_decay):
    corr_one = 1.0 - beta_one**adam_step
    corr_two = 1.0 - beta_two**adam_step
    first_new = beta_one * first + (1.0 - beta_one) * gradient
    second_new = beta_two * second + (1.0 - beta_two) * gradient * gradient
    direction = (
        first_new / corr_one / (jnp.sqrt(second_new / corr_two) + adam_eps) + weight_decay * master
    )
    master_new = master - learning_rate * direction
    return (master_new, first_new, second_new, master_new.astype(jnp.bfloat16))


def gather_all(piece, axis):
    count = lax.psum(1, axis)
    return lax.all_to_all(
        jnp.broadcast_to(piece[None], (count,) + piece.shape), axis, 0, 0, tiled=True
    )


def shards(
    grad_embed,
    grad_proj,
    grad_norms,
    embed_master,
    embed_first,
    embed_second,
    proj_master,
    proj_first,
    proj_second,
    norm_master,
    norm_first,
    norm_second,
):
    n_rep = lax.psum(1, "rep")
    n_shard = lax.psum(1, "shard")
    n_all = n_rep * n_shard
    rep_index = lax.axis_index("rep")

    embed_rows, width = grad_embed.shape[2:]
    proj_rows = grad_proj.shape[2]
    norm_rows, norm_cols = grad_norms.shape[2:]
    e_rows = embed_rows // n_all
    p_rows = proj_rows // n_all
    n_vals = norm_rows * norm_cols // n_all
    block_norm = norm_cols // n_shard
    rows = e_rows + p_rows + 2
    entry_count = float(embed_rows * width + proj_rows * width + norm_rows * norm_cols)

    embed_send = grad_embed[0, 0].reshape(n_all, e_rows, width)
    proj_send = grad_proj[0, 0].reshape(n_all, p_rows, width)
    norm_send = (
        grad_norms[0, 0]
        .reshape(norm_rows, n_shard, block_norm)
        .transpose(1, 0, 2)
        .reshape(n_all, 1, n_vals)
    )
    norm_send = jnp.pad(norm_send, ((0, 0), (0, 1), (0, width - n_vals)))
    send = jnp.concatenate([embed_send, proj_send, norm_send], axis=1)

    received = lax.all_to_all(send, ALL, 0, 0, tiled=True)
    reduced = jnp.sum(received.astype(jnp.float32), axis=0)

    partial = jnp.sum(reduced * reduced)
    squares = jnp.sum(gather_all(partial.reshape(1), ALL))
    rms_value = jnp.sqrt(squares / entry_count)
    clip_factor = jnp.minimum(jnp.float32(1.0), clip_rms / (rms_value + 1e-06))

    def flat_norm(x):
        return lax.dynamic_slice(x.reshape(-1), (rep_index * n_vals,), (n_vals,))

    e_piece = adamw(
        clip_factor * reduced[:e_rows],
        lax.dynamic_slice_in_dim(embed_master, rep_index * e_rows, e_rows),
        lax.dynamic_slice_in_dim(embed_first, rep_index * e_rows, e_rows),
        lax.dynamic_slice_in_dim(embed_second, rep_index * e_rows, e_rows),
        0.01,
    )[3]
    p_piece = adamw(
        clip_factor * reduced[e_rows : e_rows + p_rows],
        lax.dynamic_slice_in_dim(proj_master, rep_index * p_rows, p_rows),
        lax.dynamic_slice_in_dim(proj_first, rep_index * p_rows, p_rows),
        lax.dynamic_slice_in_dim(proj_second, rep_index * p_rows, p_rows),
        0.01,
    )[3]
    n_piece = adamw(
        clip_factor * reduced[e_rows + p_rows, :n_vals],
        flat_norm(norm_master),
        flat_norm(norm_first),
        flat_norm(norm_second),
        0.0,
    )[3]
    n_piece = jnp.pad(n_piece.reshape(1, n_vals), ((0, 1), (0, width - n_vals)))
    w_piece = jnp.concatenate([e_piece, p_piece, n_piece], axis=0)
    w_all = gather_all(w_piece, ALL)
    embed_weights = w_all[:, :e_rows].reshape(embed_rows, width)
    proj_weights = w_all[:, e_rows : e_rows + p_rows].reshape(proj_rows, width)
    norm_weights = (
        w_all[:, e_rows + p_rows, :n_vals]
        .reshape(n_shard, norm_rows, block_norm)
        .transpose(1, 0, 2)
        .reshape(norm_rows, norm_cols)
    )

    block = lax.all_gather(reduced, "rep", axis=0)
    embed_sum = block[:, :e_rows].reshape(n_rep * e_rows, width)
    proj_sum = block[:, e_rows : e_rows + p_rows].reshape(n_rep * p_rows, width)
    norm_sum = block[:, e_rows + p_rows, :n_vals].reshape(norm_rows, block_norm)

    embed_out = adamw(clip_factor * embed_sum, embed_master, embed_first, embed_second, 0.01)
    proj_out = adamw(clip_factor * proj_sum, proj_master, proj_first, proj_second, 0.01)
    norm_out = adamw(clip_factor * norm_sum, norm_master, norm_first, norm_second, 0.0)
    return (
        embed_out[0],
        embed_out[1],
        embed_out[2],
        embed_weights,
        proj_out[0],
        proj_out[1],
        proj_out[2],
        proj_weights,
        norm_out[0],
        norm_out[1],
        norm_out[2],
        norm_weights,
    )


def solution(mesh):
    return jax.shard_map(
        shards,
        mesh=mesh,
        in_specs=(
            P("rep", "shard", None, None),
            P("rep", "shard", None, None),
            P("rep", "shard", None, None),
            P("shard", None),
            P("shard", None),
            P("shard", None),
            P("shard", None),
            P("shard", None),
            P("shard", None),
            P(None, "shard"),
            P(None, "shard"),
            P(None, "shard"),
        ),
        out_specs=(
            P("shard", None),
            P("shard", None),
            P("shard", None),
            P(),
            P("shard", None),
            P("shard", None),
            P("shard", None),
            P(),
            P(None, "shard"),
            P(None, "shard"),
            P(None, "shard"),
            P(),
        ),
        check_vma=False,
    )
```

```python
import jax
import jax.numpy as jnp
from jax import lax
from jax.sharding import PartitionSpec as P

beta_one = 0.9
beta_two = 0.95
adam_step = 10.0
adam_eps = 1e-08
learning_rate = 0.002
clip_rms = 1.0

ALL = ("shard", "rep_hi", "core")
HALF = ("shard", "rep_hi")


def adamw(gradient, master, first, second, weight_decay):
    corr_one = 1.0 - beta_one**adam_step
    corr_two = 1.0 - beta_two**adam_step
    first_new = beta_one * first + (1.0 - beta_one) * gradient
    second_new = beta_two * second + (1.0 - beta_two) * gradient * gradient
    direction = (
        first_new / corr_one / (jnp.sqrt(second_new / corr_two) + adam_eps) + weight_decay * master
    )
    master_new = master - learning_rate * direction
    return (master_new, first_new, second_new, master_new.astype(jnp.bfloat16))


def gather_all(piece, axis):
    count = lax.psum(1, axis)
    return lax.all_to_all(
        jnp.broadcast_to(piece[None], (count,) + piece.shape), axis, 0, 0, tiled=True
    )


def shards(
    grad_embed,
    grad_proj,
    grad_norms,
    embed_master,
    embed_first,
    embed_second,
    proj_master,
    proj_first,
    proj_second,
    norm_master,
    norm_first,
    norm_second,
):
    n_rep = lax.psum(1, ("rep_hi", "core"))
    n_shard = lax.psum(1, "shard")
    n_all = n_rep * n_shard
    rep_index = lax.axis_index(("rep_hi", "core"))
    core = lax.axis_index("core")

    embed_rows, width = grad_embed.shape[2:]
    proj_rows = grad_proj.shape[2]
    norm_rows, norm_cols = grad_norms.shape[2:]
    e_rows = embed_rows // n_all
    p_rows = proj_rows // n_all
    n_vals = norm_rows * norm_cols // n_all
    block_norm = norm_cols // n_shard
    rows = e_rows + p_rows + 2
    entry_count = float(embed_rows * width + proj_rows * width + norm_rows * norm_cols)

    embed_send = grad_embed[0, 0].reshape(n_all, e_rows, width)
    proj_send = grad_proj[0, 0].reshape(n_all, p_rows, width)
    norm_send = (
        grad_norms[0, 0]
        .reshape(norm_rows, n_shard, block_norm)
        .transpose(1, 0, 2)
        .reshape(n_all, 1, n_vals)
    )
    norm_send = jnp.pad(norm_send, ((0, 0), (0, 1), (0, width - n_vals)))
    send = jnp.concatenate([embed_send, proj_send, norm_send], axis=1)

    received = lax.all_to_all(send, ALL, 0, 0, tiled=True)
    reduced = jnp.sum(received.astype(jnp.float32), axis=0)

    partial = jnp.sum(reduced * reduced)
    squares = jnp.sum(gather_all(partial.reshape(1), ALL))
    rms_value = jnp.sqrt(squares / entry_count)
    clip_factor = jnp.minimum(jnp.float32(1.0), clip_rms / (rms_value + 1e-06))

    def flat_norm(x):
        return lax.dynamic_slice(x.reshape(-1), (rep_index * n_vals,), (n_vals,))

    e_piece = adamw(
        clip_factor * reduced[:e_rows],
        lax.dynamic_slice_in_dim(embed_master, rep_index * e_rows, e_rows),
        lax.dynamic_slice_in_dim(embed_first, rep_index * e_rows, e_rows),
        lax.dynamic_slice_in_dim(embed_second, rep_index * e_rows, e_rows),
        0.01,
    )[3]
    p_piece = adamw(
        clip_factor * reduced[e_rows : e_rows + p_rows],
        lax.dynamic_slice_in_dim(proj_master, rep_index * p_rows, p_rows),
        lax.dynamic_slice_in_dim(proj_first, rep_index * p_rows, p_rows),
        lax.dynamic_slice_in_dim(proj_second, rep_index * p_rows, p_rows),
        0.01,
    )[3]
    n_piece = adamw(
        clip_factor * reduced[e_rows + p_rows, :n_vals],
        flat_norm(norm_master),
        flat_norm(norm_first),
        flat_norm(norm_second),
        0.0,
    )[3]
    n_piece = jnp.pad(n_piece.reshape(1, n_vals), ((0, 1), (0, width - n_vals)))
    w_piece = jnp.concatenate([e_piece, p_piece, n_piece], axis=0)
    w_mine = gather_all(w_piece, HALF)
    w_other = lax.ppermute(w_mine, "core", [(0, 1), (1, 0)])
    w_all = jnp.stack(
        [jnp.where(core == 0, w_mine, w_other), jnp.where(core == 0, w_other, w_mine)], axis=1
    ).reshape((n_all,) + w_piece.shape)
    embed_weights = w_all[:, :e_rows].reshape(embed_rows, width)
    proj_weights = w_all[:, e_rows : e_rows + p_rows].reshape(proj_rows, width)
    norm_weights = (
        w_all[:, e_rows + p_rows, :n_vals]
        .reshape(n_shard, norm_rows, block_norm)
        .transpose(1, 0, 2)
        .reshape(norm_rows, norm_cols)
    )

    block = gather_all(reduced, ("rep_hi", "core"))
    embed_sum = block[:, :e_rows].reshape(n_rep * e_rows, width)
    proj_sum = block[:, e_rows : e_rows + p_rows].reshape(n_rep * p_rows, width)
    norm_sum = block[:, e_rows + p_rows, :n_vals].reshape(norm_rows, block_norm)

    embed_out = adamw(clip_factor * embed_sum, embed_master, embed_first, embed_second, 0.01)
    proj_out = adamw(clip_factor * proj_sum, proj_master, proj_first, proj_second, 0.01)
    norm_out = adamw(clip_factor * norm_sum, norm_master, norm_first, norm_second, 0.0)
    return (
        embed_out[0],
        embed_out[1],
        embed_out[2],
        embed_weights,
        proj_out[0],
        proj_out[1],
        proj_out[2],
        proj_weights,
        norm_out[0],
        norm_out[1],
        norm_out[2],
        norm_weights,
    )


def solution(mesh):
    n_rep, n_shard = mesh.devices.shape
    fine = jax.sharding.Mesh(
        mesh.devices.reshape(n_rep // 2, 2, n_shard), ("rep_hi", "core", "shard")
    )
    rep = ("rep_hi", "core")
    return jax.shard_map(
        shards,
        mesh=fine,
        in_specs=(
            P(rep, "shard", None, None),
            P(rep, "shard", None, None),
            P(rep, "shard", None, None),
            P("shard", None),
            P("shard", None),
            P("shard", None),
            P("shard", None),
            P("shard", None),
            P("shard", None),
            P(None, "shard"),
            P(None, "shard"),
            P(None, "shard"),
        ),
        out_specs=(
            P("shard", None),
            P("shard", None),
            P("shard", None),
            P(),
            P("shard", None),
            P("shard", None),
            P("shard", None),
            P(),
            P(None, "shard"),
            P(None, "shard"),
            P(None, "shard"),
            P(),
        ),
        check_vma=False,
    )
```

```python
import jax
import jax.numpy as jnp
from jax import lax
from jax.sharding import PartitionSpec as P

beta_one = 0.9
beta_two = 0.95
adam_step = 10.0
adam_eps = 1e-08
learning_rate = 0.002
clip_rms = 1.0

ALL = ("shard", "rep_hi", "core")
HALF = ("shard", "rep_hi")
REP = ("rep_hi", "core")


def adamw(gradient, master, first, second, weight_decay):
    corr_one = 1.0 - beta_one**adam_step
    corr_two = 1.0 - beta_two**adam_step
    first_new = beta_one * first + (1.0 - beta_one) * gradient
    second_new = beta_two * second + (1.0 - beta_two) * gradient * gradient
    direction = (
        first_new / corr_one / (jnp.sqrt(second_new / corr_two) + adam_eps) + weight_decay * master
    )
    master_new = master - learning_rate * direction
    return (master_new, first_new, second_new, master_new.astype(jnp.bfloat16))


def gather_all(piece, axis):
    count = lax.psum(1, axis)
    return lax.all_to_all(
        jnp.broadcast_to(piece[None], (count,) + piece.shape), axis, 0, 0, tiled=True
    )


def shards(
    grad_embed,
    grad_proj,
    grad_norms,
    embed_master,
    embed_first,
    embed_second,
    proj_master,
    proj_first,
    proj_second,
    norm_master,
    norm_first,
    norm_second,
):
    n_rep = lax.psum(1, REP)
    n_shard = lax.psum(1, "shard")
    n_all = n_rep * n_shard
    rep_index = lax.axis_index(REP)
    core = lax.axis_index("core")

    embed_rows, width = grad_embed.shape[2:]
    proj_rows = grad_proj.shape[2]
    norm_rows, norm_cols = grad_norms.shape[2:]
    e_rows = embed_rows // n_all
    p_rows = proj_rows // n_all
    n_vals = norm_rows * norm_cols // n_all
    block_norm = norm_cols // n_shard
    rows = e_rows + p_rows + 2
    entry_count = float(embed_rows * width + proj_rows * width + norm_rows * norm_cols)

    embed_send = grad_embed[0, 0].reshape(n_all, e_rows, width)
    proj_send = grad_proj[0, 0].reshape(n_all, p_rows, width)
    norm_send = (
        grad_norms[0, 0]
        .reshape(norm_rows, n_shard, block_norm)
        .transpose(1, 0, 2)
        .reshape(n_all, 1, n_vals)
    )
    norm_send = jnp.pad(norm_send, ((0, 0), (0, 1), (0, width - n_vals)))
    send = jnp.concatenate([embed_send, proj_send, norm_send], axis=1)

    received = lax.all_to_all(send, ALL, 0, 0, tiled=True)
    reduced = jnp.sum(received.astype(jnp.float32), axis=0)
    from_back = [reduced] + [
        lax.ppermute(reduced, REP, [(i, (i + k) % n_rep) for i in range(n_rep)])
        for k in range(1, n_rep)
    ]
    by_rep = jnp.stack(from_back[:1] + from_back[:0:-1])
    block = jnp.roll(by_rep, rep_index, axis=0)

    partial = jnp.sum(reduced * reduced)
    squares = jnp.sum(gather_all(partial.reshape(1), ALL))
    rms_value = jnp.sqrt(squares / entry_count)
    clip_factor = jnp.minimum(jnp.float32(1.0), clip_rms / (rms_value + 1e-06))

    def flat_norm(x):
        return lax.dynamic_slice(x.reshape(-1), (rep_index * n_vals,), (n_vals,))

    e_piece = adamw(
        clip_factor * reduced[:e_rows],
        lax.dynamic_slice_in_dim(embed_master, rep_index * e_rows, e_rows),
        lax.dynamic_slice_in_dim(embed_first, rep_index * e_rows, e_rows),
        lax.dynamic_slice_in_dim(embed_second, rep_index * e_rows, e_rows),
        0.01,
    )[3]
    p_piece = adamw(
        clip_factor * reduced[e_rows : e_rows + p_rows],
        lax.dynamic_slice_in_dim(proj_master, rep_index * p_rows, p_rows),
        lax.dynamic_slice_in_dim(proj_first, rep_index * p_rows, p_rows),
        lax.dynamic_slice_in_dim(proj_second, rep_index * p_rows, p_rows),
        0.01,
    )[3]
    n_piece = adamw(
        clip_factor * reduced[e_rows + p_rows, :n_vals],
        flat_norm(norm_master),
        flat_norm(norm_first),
        flat_norm(norm_second),
        0.0,
    )[3]
    n_piece = jnp.pad(n_piece.reshape(1, n_vals), ((0, 1), (0, width - n_vals)))
    w_piece = jnp.concatenate([e_piece, p_piece, n_piece], axis=0)
    w_mine = gather_all(w_piece, HALF)
    w_other = lax.ppermute(w_mine, "core", [(0, 1), (1, 0)])

    def interleave(lo, hi):
        mine, other = w_mine[:, lo:hi], w_other[:, lo:hi]
        pair = [jnp.where(core == 0, mine, other), jnp.where(core == 0, other, mine)]
        return jnp.stack(pair, axis=1).reshape((n_all, hi - lo) + w_piece.shape[1:])

    embed_weights = interleave(0, e_rows).reshape(embed_rows, width)
    proj_weights = interleave(e_rows, e_rows + p_rows).reshape(proj_rows, width)
    norm_weights = (
        interleave(e_rows + p_rows, e_rows + p_rows + 1)[:, 0, :n_vals]
        .reshape(n_shard, norm_rows, block_norm)
        .transpose(1, 0, 2)
        .reshape(norm_rows, norm_cols)
    )

    embed_sum = block[:, :e_rows].reshape(n_rep * e_rows, width)
    proj_sum = block[:, e_rows : e_rows + p_rows].reshape(n_rep * p_rows, width)
    norm_sum = block[:, e_rows + p_rows, :n_vals].reshape(norm_rows, block_norm)

    embed_out = adamw(clip_factor * embed_sum, embed_master, embed_first, embed_second, 0.01)
    proj_out = adamw(clip_factor * proj_sum, proj_master, proj_first, proj_second, 0.01)
    norm_out = adamw(clip_factor * norm_sum, norm_master, norm_first, norm_second, 0.0)
    return (
        embed_out[0],
        embed_out[1],
        embed_out[2],
        embed_weights,
        proj_out[0],
        proj_out[1],
        proj_out[2],
        proj_weights,
        norm_out[0],
        norm_out[1],
        norm_out[2],
        norm_weights,
    )


def solution(mesh):
    n_rep, n_shard = mesh.devices.shape
    fine = jax.sharding.Mesh(
        mesh.devices.reshape(n_rep // 2, 2, n_shard), ("rep_hi", "core", "shard")
    )
    rep = ("rep_hi", "core")
    return jax.shard_map(
        shards,
        mesh=fine,
        in_specs=(
            P(rep, "shard", None, None),
            P(rep, "shard", None, None),
            P(rep, "shard", None, None),
            P("shard", None),
            P("shard", None),
            P("shard", None),
            P("shard", None),
            P("shard", None),
            P("shard", None),
            P(None, "shard"),
            P(None, "shard"),
            P(None, "shard"),
        ),
        out_specs=(
            P("shard", None),
            P("shard", None),
            P("shard", None),
            P(),
            P("shard", None),
            P("shard", None),
            P("shard", None),
            P(),
            P(None, "shard"),
            P(None, "shard"),
            P(None, "shard"),
            P(),
        ),
        check_vma=False,
    )
```

```python
import jax
import jax.numpy as jnp
from jax import lax
from jax.sharding import PartitionSpec as P

beta_one = 0.9
beta_two = 0.95
adam_step = 10.0
adam_eps = 1e-08
learning_rate = 0.002
clip_rms = 1.0

ALL = ("shard", "rep_hi", "core")
HALF = ("shard", "rep_hi")
REP = ("rep_hi", "core")


def adamw(gradient, master, first, second, weight_decay):
    corr_one = 1.0 - beta_one**adam_step
    corr_two = 1.0 - beta_two**adam_step
    first_new = beta_one * first + (1.0 - beta_one) * gradient
    second_new = beta_two * second + (1.0 - beta_two) * gradient * gradient
    direction = (
        first_new / corr_one / (jnp.sqrt(second_new / corr_two) + adam_eps) + weight_decay * master
    )
    master_new = master - learning_rate * direction
    return (master_new, first_new, second_new, master_new.astype(jnp.bfloat16))


def gather_all(piece, axis):
    count = lax.psum(1, axis)
    return lax.all_to_all(
        jnp.broadcast_to(piece[None], (count,) + piece.shape), axis, 0, 0, tiled=True
    )


def shards(
    grad_embed,
    grad_proj,
    grad_norms,
    embed_master,
    embed_first,
    embed_second,
    proj_master,
    proj_first,
    proj_second,
    norm_master,
    norm_first,
    norm_second,
):
    n_rep = lax.psum(1, ("rep_hi", "core"))
    n_shard = lax.psum(1, "shard")
    n_all = n_rep * n_shard
    rep_index = lax.axis_index(("rep_hi", "core"))
    core = lax.axis_index("core")

    embed_rows, width = grad_embed.shape[2:]
    proj_rows = grad_proj.shape[2]
    norm_rows, norm_cols = grad_norms.shape[2:]
    e_rows = embed_rows // n_all
    p_rows = proj_rows // n_all
    n_vals = norm_rows * norm_cols // n_all
    block_norm = norm_cols // n_shard
    rows = e_rows + p_rows + 2
    entry_count = float(embed_rows * width + proj_rows * width + norm_rows * norm_cols)

    embed_send = grad_embed[0, 0].reshape(n_all, e_rows, width)
    proj_send = grad_proj[0, 0].reshape(n_all, p_rows, width)
    norm_send = (
        grad_norms[0, 0]
        .reshape(norm_rows, n_shard, block_norm)
        .transpose(1, 0, 2)
        .reshape(n_all, 1, n_vals)
    )
    norm_send = jnp.pad(norm_send, ((0, 0), (0, 1), (0, width - n_vals)))
    send = jnp.concatenate([embed_send, proj_send, norm_send], axis=1)

    received = lax.all_to_all(send, ALL, 0, 0, tiled=True)
    reduced = jnp.sum(received.astype(jnp.float32), axis=0)

    block = gather_all(reduced, REP)
    embed_sum = block[:, :e_rows].reshape(n_rep * e_rows, width)
    proj_sum = block[:, e_rows : e_rows + p_rows].reshape(n_rep * p_rows, width)
    norm_sum = block[:, e_rows + p_rows, :n_vals].reshape(norm_rows, block_norm)
    partial = jnp.sum(block * block)
    squares = jnp.sum(gather_all(partial.reshape(1), "shard"))
    rms_value = jnp.sqrt(squares / entry_count)
    clip_factor = jnp.minimum(jnp.float32(1.0), clip_rms / (rms_value + 1e-06))

    embed_out = adamw(clip_factor * embed_sum, embed_master, embed_first, embed_second, 0.01)
    proj_out = adamw(clip_factor * proj_sum, proj_master, proj_first, proj_second, 0.01)
    norm_out = adamw(clip_factor * norm_sum, norm_master, norm_first, norm_second, 0.0)
    flat_weights = norm_out[3].reshape(-1)
    w_piece = jnp.concatenate(
        [
            lax.dynamic_slice_in_dim(embed_out[3], rep_index * e_rows, e_rows),
            lax.dynamic_slice_in_dim(proj_out[3], rep_index * p_rows, p_rows),
            jnp.pad(
                lax.dynamic_slice(flat_weights, (rep_index * n_vals,), (n_vals,)).reshape(1, n_vals),
                ((0, 1), (0, width - n_vals)),
            ),
        ],
        axis=0,
    )
    w_mine = gather_all(w_piece, HALF)
    w_other = lax.ppermute(w_mine, "core", [(0, 1), (1, 0)])

    def interleave(lo, hi):
        mine, other = w_mine[:, lo:hi], w_other[:, lo:hi]
        pair = [jnp.where(core == 0, mine, other), jnp.where(core == 0, other, mine)]
        return jnp.stack(pair, axis=1).reshape((n_all, hi - lo) + w_piece.shape[1:])

    embed_weights = interleave(0, e_rows).reshape(embed_rows, width)
    proj_weights = interleave(e_rows, e_rows + p_rows).reshape(proj_rows, width)
    norm_weights = (
        interleave(e_rows + p_rows, e_rows + p_rows + 1)[:, 0, :n_vals]
        .reshape(n_shard, norm_rows, block_norm)
        .transpose(1, 0, 2)
        .reshape(norm_rows, norm_cols)
    )
    return (
        embed_out[0],
        embed_out[1],
        embed_out[2],
        embed_weights,
        proj_out[0],
        proj_out[1],
        proj_out[2],
        proj_weights,
        norm_out[0],
        norm_out[1],
        norm_out[2],
        norm_weights,
    )


def solution(mesh):
    n_rep, n_shard = mesh.devices.shape
    fine = jax.sharding.Mesh(
        mesh.devices.reshape(n_rep // 2, 2, n_shard), ("rep_hi", "core", "shard")
    )
    rep = ("rep_hi", "core")
    return jax.shard_map(
        shards,
        mesh=fine,
        in_specs=(
            P(rep, "shard", None, None),
            P(rep, "shard", None, None),
            P(rep, "shard", None, None),
            P("shard", None),
            P("shard", None),
            P("shard", None),
            P("shard", None),
            P("shard", None),
            P("shard", None),
            P(None, "shard"),
            P(None, "shard"),
            P(None, "shard"),
        ),
        out_specs=(
            P("shard", None),
            P("shard", None),
            P("shard", None),
            P(),
            P("shard", None),
            P("shard", None),
            P("shard", None),
            P(),
            P(None, "shard"),
            P(None, "shard"),
            P(None, "shard"),
            P(),
        ),
        check_vma=False,
    )
```

```python
import jax
import jax.numpy as jnp
from jax import lax
from jax.sharding import PartitionSpec as P

beta_one = 0.9
beta_two = 0.95
adam_step = 10.0
adam_eps = 1e-08
learning_rate = 0.002
clip_rms = 1.0

ALL = ("shard", "rep_hi", "core")
HALF = ("shard", "rep_hi")
REP = ("rep_hi", "core")


def adamw(gradient, master, first, second, weight_decay):
    corr_one = 1.0 - beta_one**adam_step
    corr_two = 1.0 - beta_two**adam_step
    first_new = beta_one * first + (1.0 - beta_one) * gradient
    second_new = beta_two * second + (1.0 - beta_two) * gradient * gradient
    direction = (
        first_new / corr_one / (jnp.sqrt(second_new / corr_two) + adam_eps) + weight_decay * master
    )
    master_new = master - learning_rate * direction
    return (master_new, first_new, second_new, master_new.astype(jnp.bfloat16))


def gather_all(piece, axis):
    count = lax.psum(1, axis)
    return lax.all_to_all(
        jnp.broadcast_to(piece[None], (count,) + piece.shape), axis, 0, 0, tiled=True
    )


def shards(
    grad_embed,
    grad_proj,
    grad_norms,
    embed_master,
    embed_first,
    embed_second,
    proj_master,
    proj_first,
    proj_second,
    norm_master,
    norm_first,
    norm_second,
):
    n_rep = lax.psum(1, ("rep_hi", "core"))
    n_shard = lax.psum(1, "shard")
    n_all = n_rep * n_shard
    rep_index = lax.axis_index(("rep_hi", "core"))
    core = lax.axis_index("core")

    embed_rows, width = grad_embed.shape[2:]
    proj_rows = grad_proj.shape[2]
    norm_rows, norm_cols = grad_norms.shape[2:]
    e_rows = embed_rows // n_all
    p_rows = proj_rows // n_all
    n_vals = norm_rows * norm_cols // n_all
    block_norm = norm_cols // n_shard
    rows = e_rows + p_rows + 2
    entry_count = float(embed_rows * width + proj_rows * width + norm_rows * norm_cols)

    embed_send = grad_embed[0, 0].reshape(n_all, e_rows, width)
    proj_send = grad_proj[0, 0].reshape(n_all, p_rows, width)
    norm_send = (
        grad_norms[0, 0]
        .reshape(norm_rows, n_shard, block_norm)
        .transpose(1, 0, 2)
        .reshape(n_all, 1, n_vals)
    )
    norm_send = jnp.pad(norm_send, ((0, 0), (0, 1), (0, width - n_vals)))
    send = jnp.concatenate([embed_send, proj_send, norm_send], axis=1)

    received = lax.all_to_all(send, ALL, 0, 0, tiled=True)
    reduced = jnp.sum(received.astype(jnp.float32), axis=0)

    half_block = gather_all(reduced, "rep_hi")
    half_other = lax.ppermute(half_block, "core", [(0, 1), (1, 0)])
    block = jnp.stack(
        [jnp.where(core == 0, half_block, half_other), jnp.where(core == 0, half_other, half_block)],
        axis=1,
    ).reshape((n_rep,) + reduced.shape)
    embed_sum = block[:, :e_rows].reshape(n_rep * e_rows, width)
    proj_sum = block[:, e_rows : e_rows + p_rows].reshape(n_rep * p_rows, width)
    norm_sum = block[:, e_rows + p_rows, :n_vals].reshape(norm_rows, block_norm)
    partial = jnp.sum(block * block)
    squares = jnp.sum(gather_all(partial.reshape(1), "shard"))
    rms_value = jnp.sqrt(squares / entry_count)
    clip_factor = jnp.minimum(jnp.float32(1.0), clip_rms / (rms_value + 1e-06))

    embed_out = adamw(clip_factor * embed_sum, embed_master, embed_first, embed_second, 0.01)
    proj_out = adamw(clip_factor * proj_sum, proj_master, proj_first, proj_second, 0.01)
    norm_out = adamw(clip_factor * norm_sum, norm_master, norm_first, norm_second, 0.0)
    flat_weights = norm_out[3].reshape(-1)
    w_piece = jnp.concatenate(
        [
            lax.dynamic_slice_in_dim(embed_out[3], rep_index * e_rows, e_rows),
            lax.dynamic_slice_in_dim(proj_out[3], rep_index * p_rows, p_rows),
            jnp.pad(
                lax.dynamic_slice(flat_weights, (rep_index * n_vals,), (n_vals,)).reshape(1, n_vals),
                ((0, 1), (0, width - n_vals)),
            ),
        ],
        axis=0,
    )
    w_mine = gather_all(w_piece, HALF)
    w_other = lax.ppermute(w_mine, "core", [(0, 1), (1, 0)])

    def interleave(lo, hi):
        mine, other = w_mine[:, lo:hi], w_other[:, lo:hi]
        pair = [jnp.where(core == 0, mine, other), jnp.where(core == 0, other, mine)]
        return jnp.stack(pair, axis=1).reshape((n_all, hi - lo) + w_piece.shape[1:])

    embed_weights = interleave(0, e_rows).reshape(embed_rows, width)
    proj_weights = interleave(e_rows, e_rows + p_rows).reshape(proj_rows, width)
    norm_weights = (
        interleave(e_rows + p_rows, e_rows + p_rows + 1)[:, 0, :n_vals]
        .reshape(n_shard, norm_rows, block_norm)
        .transpose(1, 0, 2)
        .reshape(norm_rows, norm_cols)
    )
    return (
        embed_out[0],
        embed_out[1],
        embed_out[2],
        embed_weights,
        proj_out[0],
        proj_out[1],
        proj_out[2],
        proj_weights,
        norm_out[0],
        norm_out[1],
        norm_out[2],
        norm_weights,
    )


def solution(mesh):
    n_rep, n_shard = mesh.devices.shape
    fine = jax.sharding.Mesh(
        mesh.devices.reshape(n_rep // 2, 2, n_shard), ("rep_hi", "core", "shard")
    )
    rep = ("rep_hi", "core")
    return jax.shard_map(
        shards,
        mesh=fine,
        in_specs=(
            P(rep, "shard", None, None),
            P(rep, "shard", None, None),
            P(rep, "shard", None, None),
            P("shard", None),
            P("shard", None),
            P("shard", None),
            P("shard", None),
            P("shard", None),
            P("shard", None),
            P(None, "shard"),
            P(None, "shard"),
            P(None, "shard"),
        ),
        out_specs=(
            P("shard", None),
            P("shard", None),
            P("shard", None),
            P(),
            P("shard", None),
            P("shard", None),
            P("shard", None),
            P(),
            P(None, "shard"),
            P(None, "shard"),
            P(None, "shard"),
            P(),
        ),
        check_vma=False,
    )
```

```python
import jax
import jax.numpy as jnp
from jax import lax
from jax.sharding import PartitionSpec as P

beta_one = 0.9
beta_two = 0.95
adam_step = 10.0
adam_eps = 1e-08
learning_rate = 0.002
clip_rms = 1.0

ALL = ("shard", "rep_hi", "core")
HALF = ("shard", "rep_hi")
REP = ("rep_hi", "core")


def adamw(gradient, master, first, second, weight_decay):
    corr_one = 1.0 - beta_one**adam_step
    corr_two = 1.0 - beta_two**adam_step
    first_new = beta_one * first + (1.0 - beta_one) * gradient
    second_new = beta_two * second + (1.0 - beta_two) * gradient * gradient
    direction = (
        first_new / corr_one / (jnp.sqrt(second_new / corr_two) + adam_eps) + weight_decay * master
    )
    master_new = master - learning_rate * direction
    return (master_new, first_new, second_new, master_new.astype(jnp.bfloat16))


def gather_all(piece, axis):
    count = lax.psum(1, axis)
    return lax.all_to_all(
        jnp.broadcast_to(piece[None], (count,) + piece.shape), axis, 0, 0, tiled=True
    )


def shards(
    grad_embed,
    grad_proj,
    grad_norms,
    embed_master,
    embed_first,
    embed_second,
    proj_master,
    proj_first,
    proj_second,
    norm_master,
    norm_first,
    norm_second,
):
    n_rep = lax.psum(1, ("rep_hi", "core"))
    n_shard = lax.psum(1, "shard")
    n_all = n_rep * n_shard
    rep_index = lax.axis_index(("rep_hi", "core"))
    core = lax.axis_index("core")

    embed_rows, width = grad_embed.shape[2:]
    proj_rows = grad_proj.shape[2]
    norm_rows, norm_cols = grad_norms.shape[2:]
    e_rows = embed_rows // n_all
    p_rows = proj_rows // n_all
    n_vals = norm_rows * norm_cols // n_all
    block_norm = norm_cols // n_shard
    rows = e_rows + p_rows + 2
    entry_count = float(embed_rows * width + proj_rows * width + norm_rows * norm_cols)

    embed_send = grad_embed[0, 0].reshape(n_all, e_rows, width)
    proj_send = grad_proj[0, 0].reshape(n_all, p_rows, width)
    norm_send = (
        grad_norms[0, 0]
        .reshape(norm_rows, n_shard, block_norm)
        .transpose(1, 0, 2)
        .reshape(n_all, 1, n_vals)
    )
    norm_send = jnp.pad(norm_send, ((0, 0), (0, 1), (0, width - n_vals)))
    send = jnp.concatenate([embed_send, proj_send, norm_send], axis=1)

    received = lax.all_to_all(send, ALL, 0, 0, tiled=True)
    reduced = jnp.sum(received.astype(jnp.float32), axis=0)

    half_block = gather_all(reduced, "rep_hi")
    half_other = lax.ppermute(half_block, "core", [(0, 1), (1, 0)])
    block = jnp.stack(
        [jnp.where(core == 0, half_block, half_other), jnp.where(core == 0, half_other, half_block)],
        axis=1,
    ).reshape((n_rep,) + reduced.shape)
    embed_sum = block[:, :e_rows].reshape(n_rep * e_rows, width)
    proj_sum = block[:, e_rows : e_rows + p_rows].reshape(n_rep * p_rows, width)
    norm_sum = block[:, e_rows + p_rows, :n_vals].reshape(norm_rows, block_norm)
    partial = jnp.sum(block * block)
    squares = jnp.sum(gather_all(partial.reshape(1), "shard"))
    rms_value = jnp.sqrt(squares / entry_count)
    clip_factor = jnp.minimum(jnp.float32(1.0), clip_rms / (rms_value + 1e-06))

    def flat_norm(x):
        return lax.dynamic_slice(x.reshape(-1), (rep_index * n_vals,), (n_vals,))

    e_piece = adamw(
        clip_factor * reduced[:e_rows],
        lax.dynamic_slice_in_dim(embed_master, rep_index * e_rows, e_rows),
        lax.dynamic_slice_in_dim(embed_first, rep_index * e_rows, e_rows),
        lax.dynamic_slice_in_dim(embed_second, rep_index * e_rows, e_rows),
        0.01,
    )[3]
    p_piece = adamw(
        clip_factor * reduced[e_rows : e_rows + p_rows],
        lax.dynamic_slice_in_dim(proj_master, rep_index * p_rows, p_rows),
        lax.dynamic_slice_in_dim(proj_first, rep_index * p_rows, p_rows),
        lax.dynamic_slice_in_dim(proj_second, rep_index * p_rows, p_rows),
        0.01,
    )[3]
    n_piece = adamw(
        clip_factor * reduced[e_rows + p_rows, :n_vals],
        flat_norm(norm_master),
        flat_norm(norm_first),
        flat_norm(norm_second),
        0.0,
    )[3]
    n_piece = jnp.pad(n_piece.reshape(1, n_vals), ((0, 1), (0, width - n_vals)))
    w_piece = jnp.concatenate([e_piece, p_piece, n_piece], axis=0)
    w_mine = gather_all(w_piece, HALF)
    w_other = lax.ppermute(w_mine, "core", [(0, 1), (1, 0)])

    def interleave(lo, hi):
        mine, other = w_mine[:, lo:hi], w_other[:, lo:hi]
        pair = [jnp.where(core == 0, mine, other), jnp.where(core == 0, other, mine)]
        return jnp.stack(pair, axis=1).reshape((n_all, hi - lo) + w_piece.shape[1:])

    embed_weights = interleave(0, e_rows).reshape(embed_rows, width)
    proj_weights = interleave(e_rows, e_rows + p_rows).reshape(proj_rows, width)
    norm_weights = (
        interleave(e_rows + p_rows, e_rows + p_rows + 1)[:, 0, :n_vals]
        .reshape(n_shard, norm_rows, block_norm)
        .transpose(1, 0, 2)
        .reshape(norm_rows, norm_cols)
    )

    embed_out = adamw(clip_factor * embed_sum, embed_master, embed_first, embed_second, 0.01)
    proj_out = adamw(clip_factor * proj_sum, proj_master, proj_first, proj_second, 0.01)
    norm_out = adamw(clip_factor * norm_sum, norm_master, norm_first, norm_second, 0.0)
    return (
        embed_out[0],
        embed_out[1],
        embed_out[2],
        embed_weights,
        proj_out[0],
        proj_out[1],
        proj_out[2],
        proj_weights,
        norm_out[0],
        norm_out[1],
        norm_out[2],
        norm_weights,
    )


def solution(mesh):
    n_rep, n_shard = mesh.devices.shape
    fine = jax.sharding.Mesh(
        mesh.devices.reshape(n_rep // 2, 2, n_shard), ("rep_hi", "core", "shard")
    )
    rep = ("rep_hi", "core")
    return jax.shard_map(
        shards,
        mesh=fine,
        in_specs=(
            P(rep, "shard", None, None),
            P(rep, "shard", None, None),
            P(rep, "shard", None, None),
            P("shard", None),
            P("shard", None),
            P("shard", None),
            P("shard", None),
            P("shard", None),
            P("shard", None),
            P(None, "shard"),
            P(None, "shard"),
            P(None, "shard"),
        ),
        out_specs=(
            P("shard", None),
            P("shard", None),
            P("shard", None),
            P(),
            P("shard", None),
            P("shard", None),
            P("shard", None),
            P(),
            P(None, "shard"),
            P(None, "shard"),
            P(None, "shard"),
            P(),
        ),
        check_vma=False,
    )
```

```python
import jax
import jax.numpy as jnp
from jax import lax
from jax.sharding import PartitionSpec as P

beta_one = 0.9
beta_two = 0.95
adam_step = 10.0
adam_eps = 1e-08
learning_rate = 0.002
clip_rms = 1.0

ALL = ("shard", "rep_hi", "core")
HALF = ("shard", "rep_hi")
REP = ("rep_hi", "core")


def adamw(gradient, master, first, second, weight_decay):
    corr_one = 1.0 - beta_one**adam_step
    corr_two = 1.0 - beta_two**adam_step
    first_new = beta_one * first + (1.0 - beta_one) * gradient
    second_new = beta_two * second + (1.0 - beta_two) * gradient * gradient
    direction = (
        first_new / corr_one / (jnp.sqrt(second_new / corr_two) + adam_eps) + weight_decay * master
    )
    master_new = master - learning_rate * direction
    return (master_new, first_new, second_new, master_new.astype(jnp.bfloat16))


def gather_all(piece, axis):
    count = lax.psum(1, axis)
    return lax.all_to_all(
        jnp.broadcast_to(piece[None], (count,) + piece.shape), axis, 0, 0, tiled=True
    )


def shards(
    grad_embed,
    grad_proj,
    grad_norms,
    embed_master,
    embed_first,
    embed_second,
    proj_master,
    proj_first,
    proj_second,
    norm_master,
    norm_first,
    norm_second,
):
    n_rep = lax.psum(1, ("rep_hi", "core"))
    n_shard = lax.psum(1, "shard")
    n_all = n_rep * n_shard
    rep_index = lax.axis_index(("rep_hi", "core"))
    core = lax.axis_index("core")

    embed_rows, width = grad_embed.shape[2:]
    proj_rows = grad_proj.shape[2]
    norm_rows, norm_cols = grad_norms.shape[2:]
    e_rows = embed_rows // n_all
    p_rows = proj_rows // n_all
    n_vals = norm_rows * norm_cols // n_all
    block_norm = norm_cols // n_shard
    rows = e_rows + p_rows + 2
    entry_count = float(embed_rows * width + proj_rows * width + norm_rows * norm_cols)

    embed_send = grad_embed[0, 0].reshape(n_all, e_rows, width)
    proj_send = grad_proj[0, 0].reshape(n_all, p_rows, width)
    norm_send = (
        grad_norms[0, 0]
        .reshape(norm_rows, n_shard, block_norm)
        .transpose(1, 0, 2)
        .reshape(n_all, 1, n_vals)
    )
    norm_send = jnp.pad(norm_send, ((0, 0), (0, 1), (0, width - n_vals)))
    send = jnp.concatenate([embed_send, proj_send, norm_send], axis=1)

    def by_core(mine, other):
        shape = (mine.shape[0], 2) + mine.shape[1:]
        slot = lax.broadcasted_iota(jnp.int32, shape, 1)
        return jnp.where(slot == core, mine[:, None], other[:, None])

    received = lax.all_to_all(send, ALL, 0, 0, tiled=True)
    reduced = jnp.sum(received.astype(jnp.float32), axis=0)

    half_block = gather_all(reduced, "rep_hi")
    half_other = lax.ppermute(half_block, "core", [(0, 1), (1, 0)])
    block = by_core(half_block, half_other).reshape((n_rep,) + reduced.shape)
    embed_sum = block[:, :e_rows].reshape(n_rep * e_rows, width)
    proj_sum = block[:, e_rows : e_rows + p_rows].reshape(n_rep * p_rows, width)
    norm_sum = block[:, e_rows + p_rows, :n_vals].reshape(norm_rows, block_norm)
    partial = jnp.sum(block * block)
    squares = jnp.sum(gather_all(partial.reshape(1), "shard"))
    rms_value = jnp.sqrt(squares / entry_count)
    clip_factor = jnp.minimum(jnp.float32(1.0), clip_rms / (rms_value + 1e-06))

    def flat_norm(x):
        return lax.dynamic_slice(x.reshape(-1), (rep_index * n_vals,), (n_vals,))

    e_piece = adamw(
        clip_factor * reduced[:e_rows],
        lax.dynamic_slice_in_dim(embed_master, rep_index * e_rows, e_rows),
        lax.dynamic_slice_in_dim(embed_first, rep_index * e_rows, e_rows),
        lax.dynamic_slice_in_dim(embed_second, rep_index * e_rows, e_rows),
        0.01,
    )[3]
    p_piece = adamw(
        clip_factor * reduced[e_rows : e_rows + p_rows],
        lax.dynamic_slice_in_dim(proj_master, rep_index * p_rows, p_rows),
        lax.dynamic_slice_in_dim(proj_first, rep_index * p_rows, p_rows),
        lax.dynamic_slice_in_dim(proj_second, rep_index * p_rows, p_rows),
        0.01,
    )[3]
    n_piece = adamw(
        clip_factor * reduced[e_rows + p_rows, :n_vals],
        flat_norm(norm_master),
        flat_norm(norm_first),
        flat_norm(norm_second),
        0.0,
    )[3]
    n_piece = jnp.pad(n_piece.reshape(1, n_vals), ((0, 1), (0, width - n_vals)))
    w_piece = jnp.concatenate([e_piece, p_piece, n_piece], axis=0)
    w_mine = gather_all(w_piece, HALF)
    w_other = lax.ppermute(w_mine, "core", [(0, 1), (1, 0)])

    def interleave(lo, hi):
        return by_core(w_mine[:, lo:hi], w_other[:, lo:hi]).reshape(
            (n_all, hi - lo) + w_piece.shape[1:]
        )

    embed_weights = interleave(0, e_rows).reshape(embed_rows, width)
    proj_weights = interleave(e_rows, e_rows + p_rows).reshape(proj_rows, width)
    norm_weights = (
        interleave(e_rows + p_rows, e_rows + p_rows + 1)[:, 0, :n_vals]
        .reshape(n_shard, norm_rows, block_norm)
        .transpose(1, 0, 2)
        .reshape(norm_rows, norm_cols)
    )

    embed_out = adamw(clip_factor * embed_sum, embed_master, embed_first, embed_second, 0.01)
    proj_out = adamw(clip_factor * proj_sum, proj_master, proj_first, proj_second, 0.01)
    norm_out = adamw(clip_factor * norm_sum, norm_master, norm_first, norm_second, 0.0)
    return (
        embed_out[0],
        embed_out[1],
        embed_out[2],
        embed_weights,
        proj_out[0],
        proj_out[1],
        proj_out[2],
        proj_weights,
        norm_out[0],
        norm_out[1],
        norm_out[2],
        norm_weights,
    )


def solution(mesh):
    n_rep, n_shard = mesh.devices.shape
    fine = jax.sharding.Mesh(
        mesh.devices.reshape(n_rep // 2, 2, n_shard), ("rep_hi", "core", "shard")
    )
    rep = ("rep_hi", "core")
    return jax.shard_map(
        shards,
        mesh=fine,
        in_specs=(
            P(rep, "shard", None, None),
            P(rep, "shard", None, None),
            P(rep, "shard", None, None),
            P("shard", None),
            P("shard", None),
            P("shard", None),
            P("shard", None),
            P("shard", None),
            P("shard", None),
            P(None, "shard"),
            P(None, "shard"),
            P(None, "shard"),
        ),
        out_specs=(
            P("shard", None),
            P("shard", None),
            P("shard", None),
            P(),
            P("shard", None),
            P("shard", None),
            P("shard", None),
            P(),
            P(None, "shard"),
            P(None, "shard"),
            P(None, "shard"),
            P(),
        ),
        check_vma=False,
    )
```

```python
import jax
import jax.numpy as jnp
from jax import lax
from jax.sharding import PartitionSpec as P

beta_one = 0.9
beta_two = 0.95
adam_step = 10.0
adam_eps = 1e-08
learning_rate = 0.002
clip_rms = 1.0

ALL = ("shard", "rep_hi", "core")
HALF = ("shard", "rep_hi")
REP = ("rep_hi", "core")


def adamw(gradient, master, first, second, weight_decay):
    corr_one = 1.0 - beta_one**adam_step
    corr_two = 1.0 - beta_two**adam_step
    first_new = beta_one * first + (1.0 - beta_one) * gradient
    second_new = beta_two * second + (1.0 - beta_two) * gradient * gradient
    direction = (
        first_new / corr_one / (jnp.sqrt(second_new / corr_two) + adam_eps) + weight_decay * master
    )
    master_new = master - learning_rate * direction
    return (master_new, first_new, second_new, master_new.astype(jnp.bfloat16))


def gather_all(piece, axis):
    count = lax.psum(1, axis)
    return lax.all_to_all(
        jnp.broadcast_to(piece[None], (count,) + piece.shape), axis, 0, 0, tiled=True
    )


def shards(
    grad_embed,
    grad_proj,
    grad_norms,
    embed_master,
    embed_first,
    embed_second,
    proj_master,
    proj_first,
    proj_second,
    norm_master,
    norm_first,
    norm_second,
):
    n_rep = lax.psum(1, ("rep_hi", "core"))
    n_shard = lax.psum(1, "shard")
    n_all = n_rep * n_shard
    rep_index = lax.axis_index(("rep_hi", "core"))
    core = lax.axis_index("core")

    embed_rows, width = grad_embed.shape[2:]
    proj_rows = grad_proj.shape[2]
    norm_rows, norm_cols = grad_norms.shape[2:]
    e_rows = embed_rows // n_all
    p_rows = proj_rows // n_all
    n_vals = norm_rows * norm_cols // n_all
    block_norm = norm_cols // n_shard
    rows = e_rows + p_rows + 2
    entry_count = float(embed_rows * width + proj_rows * width + norm_rows * norm_cols)

    embed_send = grad_embed[0, 0].reshape(n_all, e_rows, width)
    proj_send = grad_proj[0, 0].reshape(n_all, p_rows, width)
    norm_send = (
        grad_norms[0, 0]
        .reshape(norm_rows, n_shard, block_norm)
        .transpose(1, 0, 2)
        .reshape(n_all, 1, n_vals)
    )
    norm_send = jnp.pad(norm_send, ((0, 0), (0, 1), (0, width - n_vals)))
    send = jnp.concatenate([embed_send, proj_send, norm_send], axis=1)

    received = lax.all_to_all(send, ALL, 0, 0, tiled=True)
    reduced = jnp.sum(received.astype(jnp.float32), axis=0)

    half_block = gather_all(reduced, "rep_hi")
    half_other = lax.ppermute(half_block, "core", [(0, 1), (1, 0)])
    block = jnp.stack(
        [jnp.where(core == 0, half_block, half_other), jnp.where(core == 0, half_other, half_block)],
        axis=1,
    ).reshape((n_rep,) + reduced.shape)
    embed_sum = block[:, :e_rows].reshape(n_rep * e_rows, width)
    proj_sum = block[:, e_rows : e_rows + p_rows].reshape(n_rep * p_rows, width)
    norm_sum = block[:, e_rows + p_rows, :n_vals].reshape(norm_rows, block_norm)
    partial = jnp.sum(block * block)
    squares = jnp.sum(gather_all(partial.reshape(1), "shard"))
    rms_value = jnp.sqrt(squares / entry_count)
    clip_factor = jnp.minimum(jnp.float32(1.0), clip_rms / (rms_value + 1e-06))

    def flat_norm(x):
        return lax.dynamic_slice(x.reshape(-1), (rep_index * n_vals,), (n_vals,))

    e_piece = adamw(
        clip_factor * reduced[:e_rows],
        lax.dynamic_slice_in_dim(embed_master, rep_index * e_rows, e_rows),
        lax.dynamic_slice_in_dim(embed_first, rep_index * e_rows, e_rows),
        lax.dynamic_slice_in_dim(embed_second, rep_index * e_rows, e_rows),
        0.01,
    )[3]
    p_piece = adamw(
        clip_factor * reduced[e_rows : e_rows + p_rows],
        lax.dynamic_slice_in_dim(proj_master, rep_index * p_rows, p_rows),
        lax.dynamic_slice_in_dim(proj_first, rep_index * p_rows, p_rows),
        lax.dynamic_slice_in_dim(proj_second, rep_index * p_rows, p_rows),
        0.01,
    )[3]
    n_piece = adamw(
        clip_factor * reduced[e_rows + p_rows, :n_vals],
        flat_norm(norm_master),
        flat_norm(norm_first),
        flat_norm(norm_second),
        0.0,
    )[3]
    n_piece = jnp.pad(n_piece.reshape(1, n_vals), ((0, 1), (0, width - n_vals)))
    w_piece = jnp.concatenate([e_piece, p_piece, n_piece], axis=0)
    w_mine = gather_all(w_piece, HALF)
    w_other = lax.ppermute(w_mine, "core", [(0, 1), (1, 0)])

    def interleave(lo, hi):
        mine, other = w_mine[:, None, lo:hi], w_other[:, None, lo:hi]
        pair = jnp.where(
            core == 0,
            jnp.concatenate([mine, other], axis=1),
            jnp.concatenate([other, mine], axis=1),
        )
        return pair.reshape((n_all, hi - lo) + w_piece.shape[1:])

    embed_weights = interleave(0, e_rows).reshape(embed_rows, width)
    proj_weights = interleave(e_rows, e_rows + p_rows).reshape(proj_rows, width)
    norm_weights = (
        interleave(e_rows + p_rows, e_rows + p_rows + 1)[:, 0, :n_vals]
        .reshape(n_shard, norm_rows, block_norm)
        .transpose(1, 0, 2)
        .reshape(norm_rows, norm_cols)
    )

    embed_out = adamw(clip_factor * embed_sum, embed_master, embed_first, embed_second, 0.01)
    proj_out = adamw(clip_factor * proj_sum, proj_master, proj_first, proj_second, 0.01)
    norm_out = adamw(clip_factor * norm_sum, norm_master, norm_first, norm_second, 0.0)
    return (
        embed_out[0],
        embed_out[1],
        embed_out[2],
        embed_weights,
        proj_out[0],
        proj_out[1],
        proj_out[2],
        proj_weights,
        norm_out[0],
        norm_out[1],
        norm_out[2],
        norm_weights,
    )


def solution(mesh):
    n_rep, n_shard = mesh.devices.shape
    fine = jax.sharding.Mesh(
        mesh.devices.reshape(n_rep // 2, 2, n_shard), ("rep_hi", "core", "shard")
    )
    rep = ("rep_hi", "core")
    return jax.shard_map(
        shards,
        mesh=fine,
        in_specs=(
            P(rep, "shard", None, None),
            P(rep, "shard", None, None),
            P(rep, "shard", None, None),
            P("shard", None),
            P("shard", None),
            P("shard", None),
            P("shard", None),
            P("shard", None),
            P("shard", None),
            P(None, "shard"),
            P(None, "shard"),
            P(None, "shard"),
        ),
        out_specs=(
            P("shard", None),
            P("shard", None),
            P("shard", None),
            P(),
            P("shard", None),
            P("shard", None),
            P("shard", None),
            P(),
            P(None, "shard"),
            P(None, "shard"),
            P(None, "shard"),
            P(),
        ),
        check_vma=False,
    )
```

```python
import jax
import jax.numpy as jnp
from jax import lax
from jax.sharding import PartitionSpec as P

beta_one = 0.9
beta_two = 0.95
adam_step = 10.0
adam_eps = 1e-08
learning_rate = 0.002
clip_rms = 1.0

ALL = ("shard", "rep_hi", "core")
HALF = ("shard", "rep_hi")
REP = ("rep_hi", "core")


def adamw(gradient, master, first, second, weight_decay):
    corr_one = 1.0 - beta_one**adam_step
    corr_two = 1.0 - beta_two**adam_step
    first_new = beta_one * first + (1.0 - beta_one) * gradient
    second_new = beta_two * second + (1.0 - beta_two) * gradient * gradient
    direction = (
        first_new / corr_one / (jnp.sqrt(second_new / corr_two) + adam_eps) + weight_decay * master
    )
    master_new = master - learning_rate * direction
    return (master_new, first_new, second_new, master_new.astype(jnp.bfloat16))


def gather_all(piece, axis):
    count = lax.psum(1, axis)
    return lax.all_to_all(
        jnp.broadcast_to(piece[None], (count,) + piece.shape), axis, 0, 0, tiled=True
    )


def shards(
    grad_embed,
    grad_proj,
    grad_norms,
    embed_master,
    embed_first,
    embed_second,
    proj_master,
    proj_first,
    proj_second,
    norm_master,
    norm_first,
    norm_second,
):
    n_rep = lax.psum(1, ("rep_hi", "core"))
    n_shard = lax.psum(1, "shard")
    n_all = n_rep * n_shard
    rep_index = lax.axis_index(("rep_hi", "core"))
    core = lax.axis_index("core")

    embed_rows, width = grad_embed.shape[2:]
    proj_rows = grad_proj.shape[2]
    norm_rows, norm_cols = grad_norms.shape[2:]
    e_rows = embed_rows // n_all
    p_rows = proj_rows // n_all
    n_vals = norm_rows * norm_cols // n_all
    block_norm = norm_cols // n_shard
    rows = e_rows + p_rows + 2
    entry_count = float(embed_rows * width + proj_rows * width + norm_rows * norm_cols)

    embed_send = grad_embed[0, 0].reshape(n_all, e_rows, width)
    proj_send = grad_proj[0, 0].reshape(n_all, p_rows, width)
    norm_send = (
        grad_norms[0, 0]
        .reshape(norm_rows, n_shard, block_norm)
        .transpose(1, 0, 2)
        .reshape(n_all, 1, n_vals)
    )
    norm_send = jnp.pad(norm_send, ((0, 0), (0, 1), (0, width - n_vals)))
    send = jnp.concatenate([embed_send, proj_send, norm_send], axis=1)

    received = lax.all_to_all(send, ALL, 0, 0, tiled=True)
    reduced = jnp.sum(received.astype(jnp.float32), axis=0)

    half_block = gather_all(reduced, "rep_hi")
    half_other = lax.ppermute(half_block, "core", [(0, 1), (1, 0)])
    block = jnp.stack(
        [jnp.where(core == 0, half_block, half_other), jnp.where(core == 0, half_other, half_block)],
        axis=1,
    ).reshape((n_rep,) + reduced.shape)
    embed_sum = block[:, :e_rows].reshape(n_rep * e_rows, width)
    proj_sum = block[:, e_rows : e_rows + p_rows].reshape(n_rep * p_rows, width)
    norm_sum = block[:, e_rows + p_rows, :n_vals].reshape(norm_rows, block_norm)
    partial = jnp.sum(half_block * half_block)
    squares = jnp.sum(gather_all(partial.reshape(1), ("shard", "core")))
    rms_value = jnp.sqrt(squares / entry_count)
    clip_factor = jnp.minimum(jnp.float32(1.0), clip_rms / (rms_value + 1e-06))

    def flat_norm(x):
        return lax.dynamic_slice(x.reshape(-1), (rep_index * n_vals,), (n_vals,))

    e_piece = adamw(
        clip_factor * reduced[:e_rows],
        lax.dynamic_slice_in_dim(embed_master, rep_index * e_rows, e_rows),
        lax.dynamic_slice_in_dim(embed_first, rep_index * e_rows, e_rows),
        lax.dynamic_slice_in_dim(embed_second, rep_index * e_rows, e_rows),
        0.01,
    )[3]
    p_piece = adamw(
        clip_factor * reduced[e_rows : e_rows + p_rows],
        lax.dynamic_slice_in_dim(proj_master, rep_index * p_rows, p_rows),
        lax.dynamic_slice_in_dim(proj_first, rep_index * p_rows, p_rows),
        lax.dynamic_slice_in_dim(proj_second, rep_index * p_rows, p_rows),
        0.01,
    )[3]
    n_piece = adamw(
        clip_factor * reduced[e_rows + p_rows, :n_vals],
        flat_norm(norm_master),
        flat_norm(norm_first),
        flat_norm(norm_second),
        0.0,
    )[3]
    n_piece = jnp.pad(n_piece.reshape(1, n_vals), ((0, 1), (0, width - n_vals)))
    w_piece = jnp.concatenate([e_piece, p_piece, n_piece], axis=0)
    w_mine = gather_all(w_piece, HALF)
    w_other = lax.ppermute(w_mine, "core", [(0, 1), (1, 0)])

    def interleave(lo, hi):
        mine, other = w_mine[:, lo:hi], w_other[:, lo:hi]
        pair = [jnp.where(core == 0, mine, other), jnp.where(core == 0, other, mine)]
        return jnp.stack(pair, axis=1).reshape((n_all, hi - lo) + w_piece.shape[1:])

    embed_weights = interleave(0, e_rows).reshape(embed_rows, width)
    proj_weights = interleave(e_rows, e_rows + p_rows).reshape(proj_rows, width)
    norm_weights = (
        interleave(e_rows + p_rows, e_rows + p_rows + 1)[:, 0, :n_vals]
        .reshape(n_shard, norm_rows, block_norm)
        .transpose(1, 0, 2)
        .reshape(norm_rows, norm_cols)
    )

    embed_out = adamw(clip_factor * embed_sum, embed_master, embed_first, embed_second, 0.01)
    proj_out = adamw(clip_factor * proj_sum, proj_master, proj_first, proj_second, 0.01)
    norm_out = adamw(clip_factor * norm_sum, norm_master, norm_first, norm_second, 0.0)
    return (
        embed_out[0],
        embed_out[1],
        embed_out[2],
        embed_weights,
        proj_out[0],
        proj_out[1],
        proj_out[2],
        proj_weights,
        norm_out[0],
        norm_out[1],
        norm_out[2],
        norm_weights,
    )


def solution(mesh):
    n_rep, n_shard = mesh.devices.shape
    fine = jax.sharding.Mesh(
        mesh.devices.reshape(n_rep // 2, 2, n_shard), ("rep_hi", "core", "shard")
    )
    rep = ("rep_hi", "core")
    return jax.shard_map(
        shards,
        mesh=fine,
        in_specs=(
            P(rep, "shard", None, None),
            P(rep, "shard", None, None),
            P(rep, "shard", None, None),
            P("shard", None),
            P("shard", None),
            P("shard", None),
            P("shard", None),
            P("shard", None),
            P("shard", None),
            P(None, "shard"),
            P(None, "shard"),
            P(None, "shard"),
        ),
        out_specs=(
            P("shard", None),
            P("shard", None),
            P("shard", None),
            P(),
            P("shard", None),
            P("shard", None),
            P("shard", None),
            P(),
            P(None, "shard"),
            P(None, "shard"),
            P(None, "shard"),
            P(),
        ),
        check_vma=False,
    )
```

```python
import jax
import jax.numpy as jnp
from jax import lax
from jax.sharding import PartitionSpec as P

beta_one = 0.9
beta_two = 0.95
adam_step = 10.0
adam_eps = 1e-08
learning_rate = 0.002
clip_rms = 1.0

ALL = ("shard", "rep_hi", "core")
HALF = ("shard", "rep_hi")
REP = ("rep_hi", "core")


def adamw(gradient, master, first, second, weight_decay):
    corr_one = 1.0 - beta_one**adam_step
    corr_two = 1.0 - beta_two**adam_step
    first_new = beta_one * first + (1.0 - beta_one) * gradient
    second_new = beta_two * second + (1.0 - beta_two) * gradient * gradient
    direction = (
        first_new / corr_one / (jnp.sqrt(second_new / corr_two) + adam_eps) + weight_decay * master
    )
    master_new = master - learning_rate * direction
    return (master_new, first_new, second_new, master_new.astype(jnp.bfloat16))


def gather_all(piece, axis):
    count = lax.psum(1, axis)
    return lax.all_to_all(
        jnp.broadcast_to(piece[None], (count,) + piece.shape), axis, 0, 0, tiled=True
    )


def shards(
    grad_embed,
    grad_proj,
    grad_norms,
    embed_master,
    embed_first,
    embed_second,
    proj_master,
    proj_first,
    proj_second,
    norm_master,
    norm_first,
    norm_second,
):
    n_rep = lax.psum(1, ("rep_hi", "core"))
    n_shard = lax.psum(1, "shard")
    n_all = n_rep * n_shard
    rep_index = lax.axis_index(("rep_hi", "core"))
    core = lax.axis_index("core")

    embed_rows, width = grad_embed.shape[2:]
    proj_rows = grad_proj.shape[2]
    norm_rows, norm_cols = grad_norms.shape[2:]
    e_rows = embed_rows // n_all
    p_rows = proj_rows // n_all
    n_vals = norm_rows * norm_cols // n_all
    block_norm = norm_cols // n_shard
    rows = e_rows + p_rows + 2
    entry_count = float(embed_rows * width + proj_rows * width + norm_rows * norm_cols)

    embed_send = grad_embed[0, 0].reshape(n_all, e_rows, width)
    proj_send = grad_proj[0, 0].reshape(n_all, p_rows, width)
    norm_send = (
        grad_norms[0, 0]
        .reshape(norm_rows, n_shard, block_norm)
        .transpose(1, 0, 2)
        .reshape(n_all, 1, n_vals)
    )
    norm_send = jnp.pad(norm_send, ((0, 0), (0, 1), (0, width - n_vals)))
    send = jnp.concatenate([embed_send, proj_send, norm_send], axis=1)

    received = lax.all_to_all(send, ALL, 0, 0, tiled=True)
    reduced = jnp.sum(received.astype(jnp.float32), axis=0)

    half_block = gather_all(reduced, "rep_hi")
    half_other = lax.ppermute(half_block, "core", [(0, 1), (1, 0)])
    partial = jnp.sum(half_block * half_block)
    squares = jnp.sum(gather_all(partial.reshape(1), ("shard", "core")))
    rms_value = jnp.sqrt(squares / entry_count)
    clip_factor = jnp.minimum(jnp.float32(1.0), clip_rms / (rms_value + 1e-06))
    half_mine, half_other, _ = lax.optimization_barrier((half_block, half_other, clip_factor))
    block = jnp.stack(
        [jnp.where(core == 0, half_mine, half_other), jnp.where(core == 0, half_other, half_mine)],
        axis=1,
    ).reshape((n_rep,) + reduced.shape)
    embed_sum = block[:, :e_rows].reshape(n_rep * e_rows, width)
    proj_sum = block[:, e_rows : e_rows + p_rows].reshape(n_rep * p_rows, width)
    norm_sum = block[:, e_rows + p_rows, :n_vals].reshape(norm_rows, block_norm)

    def flat_norm(x):
        return lax.dynamic_slice(x.reshape(-1), (rep_index * n_vals,), (n_vals,))

    e_piece = adamw(
        clip_factor * reduced[:e_rows],
        lax.dynamic_slice_in_dim(embed_master, rep_index * e_rows, e_rows),
        lax.dynamic_slice_in_dim(embed_first, rep_index * e_rows, e_rows),
        lax.dynamic_slice_in_dim(embed_second, rep_index * e_rows, e_rows),
        0.01,
    )[3]
    p_piece = adamw(
        clip_factor * reduced[e_rows : e_rows + p_rows],
        lax.dynamic_slice_in_dim(proj_master, rep_index * p_rows, p_rows),
        lax.dynamic_slice_in_dim(proj_first, rep_index * p_rows, p_rows),
        lax.dynamic_slice_in_dim(proj_second, rep_index * p_rows, p_rows),
        0.01,
    )[3]
    n_piece = adamw(
        clip_factor * reduced[e_rows + p_rows, :n_vals],
        flat_norm(norm_master),
        flat_norm(norm_first),
        flat_norm(norm_second),
        0.0,
    )[3]
    n_piece = jnp.pad(n_piece.reshape(1, n_vals), ((0, 1), (0, width - n_vals)))
    w_piece = jnp.concatenate([e_piece, p_piece, n_piece], axis=0)
    w_mine = gather_all(w_piece, HALF)
    w_other = lax.ppermute(w_mine, "core", [(0, 1), (1, 0)])

    def interleave(lo, hi):
        mine, other = w_mine[:, lo:hi], w_other[:, lo:hi]
        pair = [jnp.where(core == 0, mine, other), jnp.where(core == 0, other, mine)]
        return jnp.stack(pair, axis=1).reshape((n_all, hi - lo) + w_piece.shape[1:])

    embed_weights = interleave(0, e_rows).reshape(embed_rows, width)
    proj_weights = interleave(e_rows, e_rows + p_rows).reshape(proj_rows, width)
    norm_weights = (
        interleave(e_rows + p_rows, e_rows + p_rows + 1)[:, 0, :n_vals]
        .reshape(n_shard, norm_rows, block_norm)
        .transpose(1, 0, 2)
        .reshape(norm_rows, norm_cols)
    )

    embed_out = adamw(clip_factor * embed_sum, embed_master, embed_first, embed_second, 0.01)
    proj_out = adamw(clip_factor * proj_sum, proj_master, proj_first, proj_second, 0.01)
    norm_out = adamw(clip_factor * norm_sum, norm_master, norm_first, norm_second, 0.0)
    return (
        embed_out[0],
        embed_out[1],
        embed_out[2],
        embed_weights,
        proj_out[0],
        proj_out[1],
        proj_out[2],
        proj_weights,
        norm_out[0],
        norm_out[1],
        norm_out[2],
        norm_weights,
    )


def solution(mesh):
    n_rep, n_shard = mesh.devices.shape
    fine = jax.sharding.Mesh(
        mesh.devices.reshape(n_rep // 2, 2, n_shard), ("rep_hi", "core", "shard")
    )
    rep = ("rep_hi", "core")
    return jax.shard_map(
        shards,
        mesh=fine,
        in_specs=(
            P(rep, "shard", None, None),
            P(rep, "shard", None, None),
            P(rep, "shard", None, None),
            P("shard", None),
            P("shard", None),
            P("shard", None),
            P("shard", None),
            P("shard", None),
            P("shard", None),
            P(None, "shard"),
            P(None, "shard"),
            P(None, "shard"),
        ),
        out_specs=(
            P("shard", None),
            P("shard", None),
            P("shard", None),
            P(),
            P("shard", None),
            P("shard", None),
            P("shard", None),
            P(),
            P(None, "shard"),
            P(None, "shard"),
            P(None, "shard"),
            P(),
        ),
        check_vma=False,
    )
```

```python
import jax
import jax.numpy as jnp
from jax import lax
from jax.sharding import PartitionSpec as P

beta_one = 0.9
beta_two = 0.95
adam_step = 10.0
adam_eps = 1e-08
learning_rate = 0.002
clip_rms = 1.0

ALL = ("shard", "rep_hi", "core")
HALF = ("shard", "rep_hi")
REP = ("rep_hi", "core")


def adamw(gradient, master, first, second, weight_decay):
    corr_one = 1.0 - beta_one**adam_step
    corr_two = 1.0 - beta_two**adam_step
    first_new = beta_one * first + (1.0 - beta_one) * gradient
    second_new = beta_two * second + (1.0 - beta_two) * gradient * gradient
    direction = (
        first_new / corr_one / (jnp.sqrt(second_new / corr_two) + adam_eps) + weight_decay * master
    )
    master_new = master - learning_rate * direction
    return (master_new, first_new, second_new, master_new.astype(jnp.bfloat16))


def gather_all(piece, axis):
    count = lax.psum(1, axis)
    return lax.all_to_all(
        jnp.broadcast_to(piece[None], (count,) + piece.shape), axis, 0, 0, tiled=True
    )


def shards(
    grad_embed,
    grad_proj,
    grad_norms,
    embed_master,
    embed_first,
    embed_second,
    proj_master,
    proj_first,
    proj_second,
    norm_master,
    norm_first,
    norm_second,
):
    n_rep = lax.psum(1, ("rep_hi", "core"))
    n_shard = lax.psum(1, "shard")
    n_all = n_rep * n_shard
    rep_index = lax.axis_index(("rep_hi", "core"))
    core = lax.axis_index("core")

    embed_rows, width = grad_embed.shape[2:]
    proj_rows = grad_proj.shape[2]
    norm_rows, norm_cols = grad_norms.shape[2:]
    e_rows = embed_rows // n_all
    p_rows = proj_rows // n_all
    n_vals = norm_rows * norm_cols // n_all
    block_norm = norm_cols // n_shard
    rows = e_rows + p_rows + 2
    entry_count = float(embed_rows * width + proj_rows * width + norm_rows * norm_cols)

    embed_send = grad_embed[0, 0].reshape(n_all, e_rows, width)
    proj_send = grad_proj[0, 0].reshape(n_all, p_rows, width)
    norm_send = (
        grad_norms[0, 0]
        .reshape(norm_rows, n_shard, block_norm)
        .transpose(1, 0, 2)
        .reshape(n_all, 1, n_vals)
    )
    norm_send = jnp.pad(norm_send, ((0, 0), (0, 1), (0, width - n_vals)))
    send = jnp.concatenate([embed_send, proj_send, norm_send], axis=1)

    received = lax.all_to_all(send, ALL, 0, 0, tiled=True)
    reduced = jnp.sum(received.astype(jnp.float32), axis=0)

    half_block = gather_all(reduced, "rep_hi")
    half_other = lax.ppermute(half_block, "core", [(0, 1), (1, 0)])

    def block_rows(lo, hi):
        mine, other = half_block[:, lo:hi], half_other[:, lo:hi]
        pair = [jnp.where(core == 0, mine, other), jnp.where(core == 0, other, mine)]
        return jnp.stack(pair, axis=1).reshape((n_rep, hi - lo) + reduced.shape[1:])

    embed_sum = block_rows(0, e_rows).reshape(n_rep * e_rows, width)
    proj_sum = block_rows(e_rows, e_rows + p_rows).reshape(n_rep * p_rows, width)
    norm_sum = block_rows(e_rows + p_rows, e_rows + p_rows + 1)[:, 0, :n_vals].reshape(
        norm_rows, block_norm
    )
    partial = jnp.sum(half_block * half_block) + jnp.sum(half_other * half_other)
    squares = jnp.sum(gather_all(partial.reshape(1), "shard"))
    rms_value = jnp.sqrt(squares / entry_count)
    clip_factor = jnp.minimum(jnp.float32(1.0), clip_rms / (rms_value + 1e-06))

    def flat_norm(x):
        return lax.dynamic_slice(x.reshape(-1), (rep_index * n_vals,), (n_vals,))

    e_piece = adamw(
        clip_factor * reduced[:e_rows],
        lax.dynamic_slice_in_dim(embed_master, rep_index * e_rows, e_rows),
        lax.dynamic_slice_in_dim(embed_first, rep_index * e_rows, e_rows),
        lax.dynamic_slice_in_dim(embed_second, rep_index * e_rows, e_rows),
        0.01,
    )[3]
    p_piece = adamw(
        clip_factor * reduced[e_rows : e_rows + p_rows],
        lax.dynamic_slice_in_dim(proj_master, rep_index * p_rows, p_rows),
        lax.dynamic_slice_in_dim(proj_first, rep_index * p_rows, p_rows),
        lax.dynamic_slice_in_dim(proj_second, rep_index * p_rows, p_rows),
        0.01,
    )[3]
    n_piece = adamw(
        clip_factor * reduced[e_rows + p_rows, :n_vals],
        flat_norm(norm_master),
        flat_norm(norm_first),
        flat_norm(norm_second),
        0.0,
    )[3]
    n_piece = jnp.pad(n_piece.reshape(1, n_vals), ((0, 1), (0, width - n_vals)))
    w_piece = jnp.concatenate([e_piece, p_piece, n_piece], axis=0)
    w_mine = gather_all(w_piece, HALF)
    w_other = lax.ppermute(w_mine, "core", [(0, 1), (1, 0)])

    def interleave(lo, hi):
        mine, other = w_mine[:, lo:hi], w_other[:, lo:hi]
        pair = [jnp.where(core == 0, mine, other), jnp.where(core == 0, other, mine)]
        return jnp.stack(pair, axis=1).reshape((n_all, hi - lo) + w_piece.shape[1:])

    embed_weights = interleave(0, e_rows).reshape(embed_rows, width)
    proj_weights = interleave(e_rows, e_rows + p_rows).reshape(proj_rows, width)
    norm_weights = (
        interleave(e_rows + p_rows, e_rows + p_rows + 1)[:, 0, :n_vals]
        .reshape(n_shard, norm_rows, block_norm)
        .transpose(1, 0, 2)
        .reshape(norm_rows, norm_cols)
    )

    embed_out = adamw(clip_factor * embed_sum, embed_master, embed_first, embed_second, 0.01)
    proj_out = adamw(clip_factor * proj_sum, proj_master, proj_first, proj_second, 0.01)
    norm_out = adamw(clip_factor * norm_sum, norm_master, norm_first, norm_second, 0.0)
    return (
        embed_out[0],
        embed_out[1],
        embed_out[2],
        embed_weights,
        proj_out[0],
        proj_out[1],
        proj_out[2],
        proj_weights,
        norm_out[0],
        norm_out[1],
        norm_out[2],
        norm_weights,
    )


def solution(mesh):
    n_rep, n_shard = mesh.devices.shape
    fine = jax.sharding.Mesh(
        mesh.devices.reshape(n_rep // 2, 2, n_shard), ("rep_hi", "core", "shard")
    )
    rep = ("rep_hi", "core")
    return jax.shard_map(
        shards,
        mesh=fine,
        in_specs=(
            P(rep, "shard", None, None),
            P(rep, "shard", None, None),
            P(rep, "shard", None, None),
            P("shard", None),
            P("shard", None),
            P("shard", None),
            P("shard", None),
            P("shard", None),
            P("shard", None),
            P(None, "shard"),
            P(None, "shard"),
            P(None, "shard"),
        ),
        out_specs=(
            P("shard", None),
            P("shard", None),
            P("shard", None),
            P(),
            P("shard", None),
            P("shard", None),
            P("shard", None),
            P(),
            P(None, "shard"),
            P(None, "shard"),
            P(None, "shard"),
            P(),
        ),
        check_vma=False,
    )
```

```python
import jax
import jax.numpy as jnp
from jax import lax
from jax.sharding import PartitionSpec as P

beta_one = 0.9
beta_two = 0.95
adam_step = 10.0
adam_eps = 1e-08
learning_rate = 0.002
clip_rms = 1.0

ALL = ("shard", "rep_hi", "core")
HALF = ("shard", "rep_hi")
REP = ("rep_hi", "core")


def adamw(gradient, master, first, second, weight_decay):
    corr_one = 1.0 - beta_one**adam_step
    corr_two = 1.0 - beta_two**adam_step
    first_new = beta_one * first + (1.0 - beta_one) * gradient
    second_new = beta_two * second + (1.0 - beta_two) * gradient * gradient
    direction = (
        first_new / corr_one / (jnp.sqrt(second_new / corr_two) + adam_eps) + weight_decay * master
    )
    master_new = master - learning_rate * direction
    return (master_new, first_new, second_new, master_new.astype(jnp.bfloat16))


def gather_all(piece, axis):
    count = lax.psum(1, axis)
    return lax.all_to_all(
        jnp.broadcast_to(piece[None], (count,) + piece.shape), axis, 0, 0, tiled=True
    )


def shards(
    grad_embed,
    grad_proj,
    grad_norms,
    embed_master,
    embed_first,
    embed_second,
    proj_master,
    proj_first,
    proj_second,
    norm_master,
    norm_first,
    norm_second,
):
    n_rep = lax.psum(1, ("rep_hi", "core"))
    n_shard = lax.psum(1, "shard")
    n_all = n_rep * n_shard
    rep_index = lax.axis_index(("rep_hi", "core"))
    core = lax.axis_index("core")

    embed_rows, width = grad_embed.shape[2:]
    proj_rows = grad_proj.shape[2]
    norm_rows, norm_cols = grad_norms.shape[2:]
    e_rows = embed_rows // n_all
    p_rows = proj_rows // n_all
    n_vals = norm_rows * norm_cols // n_all
    block_norm = norm_cols // n_shard
    rows = e_rows + p_rows + 2
    entry_count = float(embed_rows * width + proj_rows * width + norm_rows * norm_cols)

    embed_send = grad_embed[0, 0].reshape(n_all, e_rows, width)
    proj_send = grad_proj[0, 0].reshape(n_all, p_rows, width)
    norm_send = (
        grad_norms[0, 0]
        .reshape(norm_rows, n_shard, block_norm)
        .transpose(1, 0, 2)
        .reshape(n_all, 1, n_vals)
    )
    norm_send = jnp.pad(norm_send, ((0, 0), (0, 1), (0, width - n_vals)))
    send = jnp.concatenate([embed_send, proj_send, norm_send], axis=1)

    received = lax.all_to_all(send, ALL, 0, 0, tiled=True)
    reduced = jnp.sum(received.astype(jnp.float32), axis=0)

    half_block = gather_all(reduced, "rep_hi")
    half_other = lax.ppermute(half_block, "core", [(0, 1), (1, 0)])

    def block_rows(lo, hi):
        mine, other = half_block[:, lo:hi], half_other[:, lo:hi]
        pair = [jnp.where(core == 0, mine, other), jnp.where(core == 0, other, mine)]
        return jnp.stack(pair, axis=1).reshape((n_rep, hi - lo) + reduced.shape[1:])

    embed_sum = block_rows(0, e_rows).reshape(n_rep * e_rows, width)
    proj_sum = block_rows(e_rows, e_rows + p_rows).reshape(n_rep * p_rows, width)
    norm_sum = block_rows(e_rows + p_rows, e_rows + p_rows + 1)[:, 0, :n_vals].reshape(
        norm_rows, block_norm
    )
    partial = jnp.sum(half_block * half_block) + jnp.sum(half_other * half_other)
    squares = jnp.sum(gather_all(partial.reshape(1), "shard"))
    rms_value = jnp.sqrt(squares / entry_count)
    clip_factor = jnp.minimum(jnp.float32(1.0), clip_rms / (rms_value + 1e-06))

    def flat_norm(x):
        return lax.dynamic_slice(x.reshape(-1), (rep_index * n_vals,), (n_vals,))

    e_piece = adamw(
        clip_factor * reduced[:e_rows],
        lax.dynamic_slice_in_dim(embed_master, rep_index * e_rows, e_rows),
        lax.dynamic_slice_in_dim(embed_first, rep_index * e_rows, e_rows),
        lax.dynamic_slice_in_dim(embed_second, rep_index * e_rows, e_rows),
        0.01,
    )[3]
    p_piece = adamw(
        clip_factor * reduced[e_rows : e_rows + p_rows],
        lax.dynamic_slice_in_dim(proj_master, rep_index * p_rows, p_rows),
        lax.dynamic_slice_in_dim(proj_first, rep_index * p_rows, p_rows),
        lax.dynamic_slice_in_dim(proj_second, rep_index * p_rows, p_rows),
        0.01,
    )[3]
    n_piece = adamw(
        clip_factor * reduced[e_rows + p_rows, :n_vals],
        flat_norm(norm_master),
        flat_norm(norm_first),
        flat_norm(norm_second),
        0.0,
    )[3]
    n_piece = jnp.pad(n_piece.reshape(1, n_vals), ((0, 1), (0, width - n_vals)))
    w_piece = jnp.concatenate([e_piece, p_piece, n_piece], axis=0)
    w_mine = gather_all(w_piece, HALF)
    w_other = lax.ppermute(w_mine, "core", [(0, 1), (1, 0)])

    def interleave(lo, hi):
        mine, other = w_mine[:, lo:hi], w_other[:, lo:hi]
        pair = [jnp.where(core == 0, mine, other), jnp.where(core == 0, other, mine)]
        return jnp.stack(pair, axis=1).reshape((n_all, hi - lo) + w_piece.shape[1:])

    embed_weights = interleave(0, e_rows).reshape(embed_rows, width)
    proj_weights = interleave(e_rows, e_rows + p_rows).reshape(proj_rows, width)
    norm_mine, norm_other = w_mine[:, e_rows + p_rows, :n_vals], w_other[:, e_rows + p_rows, :n_vals]
    norm_pair = [
        jnp.where(core == 0, norm_mine, norm_other),
        jnp.where(core == 0, norm_other, norm_mine),
    ]
    norm_weights = (
        jnp.stack(norm_pair, axis=1)
        .reshape(n_shard, norm_rows, block_norm)
        .transpose(1, 0, 2)
        .reshape(norm_rows, norm_cols)
    )

    embed_out = adamw(clip_factor * embed_sum, embed_master, embed_first, embed_second, 0.01)
    proj_out = adamw(clip_factor * proj_sum, proj_master, proj_first, proj_second, 0.01)
    norm_out = adamw(clip_factor * norm_sum, norm_master, norm_first, norm_second, 0.0)
    return (
        embed_out[0],
        embed_out[1],
        embed_out[2],
        embed_weights,
        proj_out[0],
        proj_out[1],
        proj_out[2],
        proj_weights,
        norm_out[0],
        norm_out[1],
        norm_out[2],
        norm_weights,
    )


def solution(mesh):
    n_rep, n_shard = mesh.devices.shape
    fine = jax.sharding.Mesh(
        mesh.devices.reshape(n_rep // 2, 2, n_shard), ("rep_hi", "core", "shard")
    )
    rep = ("rep_hi", "core")
    return jax.shard_map(
        shards,
        mesh=fine,
        in_specs=(
            P(rep, "shard", None, None),
            P(rep, "shard", None, None),
            P(rep, "shard", None, None),
            P("shard", None),
            P("shard", None),
            P("shard", None),
            P("shard", None),
            P("shard", None),
            P("shard", None),
            P(None, "shard"),
            P(None, "shard"),
            P(None, "shard"),
        ),
        out_specs=(
            P("shard", None),
            P("shard", None),
            P("shard", None),
            P(),
            P("shard", None),
            P("shard", None),
            P("shard", None),
            P(),
            P(None, "shard"),
            P(None, "shard"),
            P(None, "shard"),
            P(),
        ),
        check_vma=False,
    )
```
